256 devices in a mesh: pp: 16 (over z_lo, y, core), ep: 16 (over x, z_hi).
Axes of the slice: x: 4, y: 4, z: 8 (z_hi: 4, z_lo: 2; z = z_hi * 2 + z_lo), core: 2. Of those that a mesh axis runs over, the one named last changes fastest.
Arguments:
- fwd_tokens: bfloat16 [16, 2048, 3584], P('pp', 'ep'), may hold values from -6 to 6
- fwd_routes: int32 [16, 2048, 2], P('pp', 'ep'), may hold values from 0 to 7, all different within a row; in each aligned block of 128 rows (0 to 127, 128 to 255, ..., all dimensions but the last counted through in order) at most 48 rows name the same one
- fwd_weights: float32 [16, 2048, 2], P('pp', 'ep'), may hold values from 0.2 to 1
- bwd_tokens: bfloat16 [16, 2048, 3584], P('pp', 'ep'), may hold values from -6 to 6
- bwd_grads: bfloat16 [16, 2048, 3584], P('pp', 'ep'), may hold values from -6 to 6
- bwd_routes: int32 [16, 2048, 2], P('pp', 'ep'), may hold values from 0 to 7, all different within a row; in each aligned block of 128 rows (0 to 127, 128 to 255, ..., all dimensions but the last counted through in order) at most 48 rows name the same one
- bwd_weights: float32 [16, 2048, 2], P('pp', 'ep'), may hold values from 0.2 to 1
- up_proj: bfloat16 [16, 3584, 8192], P('pp', None, 'ep'), may hold values from -0.09375 to 0.09375
- down_proj: bfloat16 [16, 8192, 3584], P('pp', 'ep'), may hold values from -0.1875 to 0.1875
Outputs:
- next_input: bfloat16 [16, 2048, 3584], P('pp', 'ep')
- prev_grad: bfloat16 [16, 2048, 3584], P('pp', 'ep')
The draws below stay inside these ranges and needn't reach their ends.
Inputs may be any that keep to these rules, and one draw needn't show every extreme that they name: `fwd_routes`: each row names 2 different experts. Among the 128 rows of one device no expert is named more than 48 times; on some devices some expert is named exactly 48 times. `bwd_routes`: as for fwd_routes.
All inputs are finite; a program needn't handle non-finite values.
Results may differ from the reference program's by a relative error of at most 0.0043.
Values may be sent and summed in bfloat16 or wider, within the bound.
No kernel may reach another device: no remote copies, remote signals or barrier semaphores. Data moves between devices by JAX's collectives and lax.ppermute only.
A program may use at most 128 MiB of HBM per device.

```python
import math
import jax
import jax.numpy as jnp
import numpy as np
from jax import lax

D = 3584
FF_DEV = 512
TOP = 2
TOK_DEV = 128
FF = 1024
EXPERTS = 8
SECTIONS = 16
TOKENS = 2048
CAP = 48
N_EP = 16


def shard_levels(key, extent, pieces, low, top_value):
    def one(dim, blocks):
        draws = jax.random.uniform(jax.random.fold_in(jax.random.fold_in(key, 6), dim), (blocks,), jnp.float32, low / len(pieces), top_value / len(pieces))
        return jnp.repeat(jnp.exp(draws), extent[dim] // blocks).reshape((-1,) + (1,) * (len(extent) - dim - 1))

    level = one(*pieces[0])
    for cut in pieces[1:]:
        level = level * one(*cut)
    return level


def routed_block(key, own, number, rows, number_of, top, limit, slope):
    order = jax.random.permutation(key, number_of)
    packed, common = portions_of(number_of, rows * top, limit, slope, True), portions_of(number_of, rows * top, limit, slope, False)
    places = jnp.arange(number_of)

    def named(tallies, offset_by):
        used = int((tallies > 0).sum())
        fixed = max(1, used // 4)
        passed = fixed + (places - fixed + offset_by * (used - fixed)) % max(1, number_of - fixed)
        return jnp.zeros((number_of,), jnp.int32).at[order[jnp.where(places < fixed, places, passed)]].set(jnp.asarray(tallies, jnp.int32))

    tallies = jnp.where(number % 4 == 0, named(packed, number // 4), named(common, number - number // 4 - 1))
    mixed = jax.random.permutation(jax.random.fold_in(own, 3), number_of)
    donor, receiver = mixed[0:number_of // 2 * 2:2], mixed[1:number_of // 2 * 2:2]
    margin = jnp.minimum(tallies[donor] - 1, limit - tallies[receiver]) // 2
    margin = jnp.where((donor == order[0]) | (receiver == order[0]) | (tallies[receiver] == 0), 0, jnp.maximum(margin, 0))
    passed = jax.random.randint(jax.random.fold_in(own, 4), (number_of // 2,), 0, 1 << 20) % (margin + 1)
    tallies = tallies.at[donor].add(-passed).at[receiver].add(passed)
    members = jnp.searchsorted(jnp.cumsum(tallies), jnp.arange(rows * top), side="right").astype(jnp.int32)
    listing = members.reshape(top, rows).T
    listing = listing[jax.random.permutation(jax.random.fold_in(own, 1), rows)]
    offset_by = jax.random.randint(jax.random.fold_in(own, 2), (rows, 1), 0, top)
    return jnp.take_along_axis(listing, (jnp.arange(top)[None, :] + offset_by) % top, axis=1)


def portions_of(amount, total, limit, slope, full):
    loads = [(1 << 20) // math.isqrt(rank ** slope) + 1 for rank in range(1, amount + 1)]
    largest = limit if full else min(limit, max(-(-total // amount), total * loads[0] // sum(loads)))
    least = 1 if total - largest >= amount - 1 else 0
    holding, spare = [largest] + [least] * (amount - 1), total - largest - least * (amount - 1)
    while spare > 0:
        free = [i for i in range(1, amount) if holding[i] < largest] or [i for i in range(1, amount) if holding[i] < limit]
        mass, remaining = sum([loads[i] for i in free]), spare
        for i in free:
            more = min(limit - holding[i], max(1, remaining * loads[i] // mass), spare)
            holding[i] = holding[i] + more
            spare = spare - more
    return np.array(holding)


def bell_draw(rng, dims, width, reach, split=(), kind=jnp.bfloat16):
    entries = width * jax.random.normal(rng, dims, jnp.float32)
    if split:
        entries = entries * shard_levels(rng, dims, split, -0.22, 0.18)
    return jnp.clip(entries, -reach, reach).astype(kind)


def setup_inputs(seed: int = 0) -> dict:
    streams_of = jax.random.split(jax.random.key(seed), 10)
    fwd_tokens = bell_draw(streams_of[0], (SECTIONS, TOKENS, D), 1.0, 6.0, ((0, 16), (1, 16)))
    fwd_routes_keys = jax.random.split(jax.random.fold_in(streams_of[1], 1), SECTIONS * TOKENS // TOK_DEV)
    fwd_routes_turns = jax.random.permutation(jax.random.fold_in(streams_of[1], 3), SECTIONS * TOKENS // TOK_DEV)
    fwd_routes = jax.vmap(lambda own, number: routed_block(jax.random.fold_in(streams_of[1], 2), own, number, TOK_DEV, EXPERTS, TOP, CAP, 2))(fwd_routes_keys, fwd_routes_turns).reshape((SECTIONS, TOKENS, TOP))
    fwd_weights = jnp.clip(0.2 + 0.8 * jax.random.uniform(streams_of[2], (SECTIONS, TOKENS, TOP), jnp.float32) ** shard_levels(streams_of[2], (SECTIONS, TOKENS, TOP), ((0, 16), (1, 16)), -0.2, 0.2), 0.2, 1.0)
    bwd_tokens = bell_draw(streams_of[3], (SECTIONS, TOKENS, D), 1.0, 6.0, ((0, 16), (1, 16)))
    bwd_grads = bell_draw(streams_of[4], (SECTIONS, TOKENS, D), 1.0, 6.0, ((0, 16), (1, 16)))
    bwd_routes_keys = jax.random.split(jax.random.fold_in(streams_of[5], 1), SECTIONS * TOKENS // TOK_DEV)
    bwd_routes_turns = jax.random.permutation(jax.random.fold_in(streams_of[5], 3), SECTIONS * TOKENS // TOK_DEV)
    bwd_routes = jax.vmap(lambda own, number: routed_block(jax.random.fold_in(streams_of[5], 2), own, number, TOK_DEV, EXPERTS, TOP, CAP, 2))(bwd_routes_keys, bwd_routes_turns).reshape((SECTIONS, TOKENS, TOP))
    bwd_weights = jnp.clip(0.2 + 0.8 * jax.random.uniform(streams_of[6], (SECTIONS, TOKENS, TOP), jnp.float32) ** shard_levels(streams_of[6], (SECTIONS, TOKENS, TOP), ((0, 16), (1, 16)), -0.2, 0.2), 0.2, 1.0)
    up_proj = bell_draw(streams_of[7], (SECTIONS, D, EXPERTS * FF), D ** -0.5, 0.09375, ((0, 16), (2, 16)))
    down_proj = bell_draw(streams_of[8], (SECTIONS, EXPERTS * FF, D), FF ** -0.5, 0.1875, ((0, 16), (1, 16)))
    return {"fwd_tokens": fwd_tokens, "fwd_routes": fwd_routes, "fwd_weights": fwd_weights, "bwd_tokens": bwd_tokens, "bwd_grads": bwd_grads, "bwd_routes": bwd_routes, "bwd_weights": bwd_weights, "up_proj": up_proj, "down_proj": down_proj}


def silu_slope(pre_act):
    sigmoid_value = jax.nn.sigmoid(pre_act)
    return sigmoid_value * (1.0 + pre_act * (1.0 - sigmoid_value))


def slot_indices(routes):
    chosen = routes.reshape(N_EP, TOK_DEV * TOP)
    onehot = (chosen[:, :, None] == jnp.arange(EXPERTS, dtype=jnp.int32)[None, None, :]).astype(jnp.int32)
    earlier = jnp.cumsum(onehot, axis=1) - onehot
    position = jnp.sum(earlier * onehot, axis=2).astype(jnp.int32)
    source = jnp.broadcast_to(jnp.arange(N_EP, dtype=jnp.int32)[:, None], chosen.shape)
    return chosen.reshape(-1), source.reshape(-1), position.reshape(-1)


def scatter_rows(values, expert_ids, source, position):
    spread = jnp.broadcast_to(values[:, None, :], (TOKENS, TOP, D)).reshape(TOKENS * TOP, D)
    buffer = jnp.zeros((EXPERTS, N_EP, CAP, D), jnp.bfloat16)
    buffer = buffer.at[expert_ids, source, position].set(spread)
    return buffer.reshape(EXPERTS, N_EP * CAP, D)


def combine(residual, results, expert_ids, source, position, route_weights):
    picked = results.reshape(EXPERTS, N_EP, CAP, D)[expert_ids, source, position]
    picked = picked.reshape(TOKENS, TOP, D).astype(jnp.float32)
    combined = residual.astype(jnp.float32) + jnp.sum(route_weights[:, :, None] * picked, axis=1)
    return combined.astype(jnp.bfloat16)


def forward_expert(operands):
    rows_in, up_part, down_part = operands
    halves = []
    for half_index in range(2):
        hidden = jax.nn.silu(jnp.dot(rows_in, up_part[:, half_index], preferred_element_type=jnp.float32)).astype(jnp.bfloat16)
        halves.append(jnp.dot(hidden, down_part[half_index], preferred_element_type=jnp.float32).astype(jnp.bfloat16))
    return (halves[0].astype(jnp.float32) + halves[1].astype(jnp.float32)).astype(jnp.bfloat16)


def backward_expert(operands):
    rows_in, grad_rows, up_part, down_part = operands
    halves = []
    for half_index in range(2):
        pre_act = jnp.dot(rows_in, up_part[:, half_index], preferred_element_type=jnp.float32)
        upstream = lax.dot_general(grad_rows, down_part[half_index], (((1,), (1,)), ((), ())), preferred_element_type=jnp.float32)
        hidden_grad = (silu_slope(pre_act) * upstream).astype(jnp.bfloat16)
        halves.append(lax.dot_general(hidden_grad, up_part[:, half_index], (((1,), (1,)), ((), ())), preferred_element_type=jnp.float32).astype(jnp.bfloat16))
    return (halves[0].astype(jnp.float32) + halves[1].astype(jnp.float32)).astype(jnp.bfloat16)


def one_section(operands):
    fwd_tokens, fwd_routes, fwd_weights, bwd_tokens, bwd_grads, bwd_routes, bwd_weights, up_proj, down_proj = operands
    up_parts = jnp.transpose(up_proj.reshape(D, EXPERTS, 2, FF_DEV), (1, 0, 2, 3))
    down_parts = down_proj.reshape(EXPERTS, 2, FF_DEV, D)
    fwd_ids, fwd_source, fwd_position = slot_indices(fwd_routes)
    fwd_buffer = scatter_rows(fwd_tokens, fwd_ids, fwd_source, fwd_position)
    fwd_results = lax.map(forward_expert, (fwd_buffer, up_parts, down_parts))
    fwd_out = combine(fwd_tokens, fwd_results, fwd_ids, fwd_source, fwd_position, fwd_weights)
    bwd_ids, bwd_source, bwd_position = slot_indices(bwd_routes)
    bwd_buffer = scatter_rows(bwd_tokens, bwd_ids, bwd_source, bwd_position)
    grad_buffer = scatter_rows(bwd_grads, bwd_ids, bwd_source, bwd_position)
    bwd_results = lax.map(backward_expert, (bwd_buffer, grad_buffer, up_parts, down_parts))
    bwd_out = combine(bwd_grads, bwd_results, bwd_ids, bwd_source, bwd_position, bwd_weights)
    return fwd_out, bwd_out


def reference(fwd_tokens, fwd_routes, fwd_weights, bwd_tokens, bwd_grads, bwd_routes, bwd_weights, up_proj, down_proj):
    fwd_all, bwd_all = lax.map(one_section, (fwd_tokens, fwd_routes, fwd_weights, bwd_tokens, bwd_grads, bwd_routes, bwd_weights, up_proj, down_proj))
    next_input = jnp.roll(fwd_all, 1, axis=0)
    prev_grad = jnp.roll(bwd_all, -1, axis=0)
    return (next_input, prev_grad)
```

```python
import jax
import jax.numpy as jnp
from jax import lax
from jax.sharding import Mesh
from jax.sharding import PartitionSpec as P

Z_PARTS = 4


def from_behind(value, axis, by):
    size = lax.axis_size(axis)
    return lax.ppermute(value, axis, [(i, (i + by) % size) for i in range(size)])


def silu_slope(pre_act):
    sigmoid_value = jax.nn.sigmoid(pre_act)
    return sigmoid_value * (1.0 + pre_act * (1.0 - sigmoid_value))


def slot_positions(chosen, expert_count):
    groups, tok_rows, route_count = chosen.shape
    onehot = (chosen[..., None] == jnp.arange(expert_count, dtype=jnp.int32)).astype(jnp.int32)
    flat_hot = onehot.reshape(groups, tok_rows * route_count, expert_count)
    earlier = jnp.cumsum(flat_hot, axis=1) - flat_hot
    return jnp.sum(earlier * flat_hot, axis=2).reshape(groups, tok_rows, route_count)


def local_slots(chosen, position, expert_class, class_count, capacity):
    column = chosen // class_count
    mine = (chosen % class_count) == expert_class
    return jnp.where(mine, column * capacity + position, -1)


def pack_rows(sources, slots, slot_total):
    table = jnp.sum(
        (slots[..., None] == jnp.arange(slot_total, dtype=jnp.int32)).astype(jnp.bfloat16), axis=2
    )
    return tuple(
        jnp.einsum("gts,gtd->gsd", table, member, preferred_element_type=jnp.float32).astype(jnp.bfloat16)
        for member in sources
    )


def weighted_partial(results, slots, route_weights):
    groups, tok_rows, route_count = slots.shape
    valid = slots >= 0
    index = jnp.where(valid, slots, 0)
    weight = jnp.where(valid, route_weights, 0.0)
    total = None
    for k in range(route_count):
        picked = jnp.take_along_axis(results, index[:, :, k, None], axis=1).astype(jnp.float32)
        term = weight[:, :, k, None] * picked
        total = term if total is None else total + term
    return total.astype(jnp.bfloat16)


def forward_work(rows, w_up, w_down):
    hidden = jax.nn.silu(jnp.dot(rows, w_up, preferred_element_type=jnp.float32)).astype(jnp.bfloat16)
    return jnp.dot(hidden, w_down, preferred_element_type=jnp.float32).astype(jnp.bfloat16)


def backward_work(rows, grad_rows, w_up, w_down):
    pre_act = jnp.dot(rows, w_up, preferred_element_type=jnp.float32)
    upstream = lax.dot_general(grad_rows, w_down, (((1,), (1,)), ((), ())), preferred_element_type=jnp.float32)
    hidden_grad = (silu_slope(pre_act) * upstream).astype(jnp.bfloat16)
    return lax.dot_general(
        hidden_grad, w_up, (((1,), (1,)), ((), ())), preferred_element_type=jnp.float32
    ).astype(jnp.bfloat16)


def to_experts(packed, x_count, capacity):
    groups, slot_total, features = packed.shape
    spread = packed.reshape(groups, x_count, capacity, features)
    got = lax.all_to_all(spread, "ex", split_axis=1, concat_axis=1, tiled=True)
    return got.reshape(groups * x_count * capacity, features)


def from_experts(rows, groups, x_count, capacity):
    features = rows.shape[-1]
    spread = rows.reshape(groups, x_count, capacity, features)
    back = lax.all_to_all(spread, "ex", split_axis=1, concat_axis=1, tiled=True)
    return back.reshape(groups, x_count * capacity, features)


def sum_back(residual, partial):
    got = lax.all_to_all(partial, "ez", split_axis=0, concat_axis=0, tiled=True)
    total = residual.astype(jnp.float32) + jnp.sum(got.astype(jnp.float32), axis=0)
    return total.astype(jnp.bfloat16)


def on_device(
    fwd_tokens,
    fwd_routes,
    fwd_weights,
    bwd_tokens,
    bwd_grads,
    bwd_routes,
    bwd_weights,
    up_proj,
    down_proj,
):
    x_count = lax.axis_size("ex")
    z_count = lax.axis_size("ez")
    ep_count = x_count * z_count
    expert_count = ep_count // 2
    class_count = expert_count // x_count
    tok_rows = fwd_tokens.shape[1]
    route_count = fwd_routes.shape[2]
    capacity = 3 * tok_rows * route_count // ep_count
    slot_total = x_count * capacity
    z_index = lax.axis_index("ez")
    expert_class = z_index // (z_count // class_count)
    w_up = up_proj[0]
    w_down = down_proj[0]

    def gather_z(value):
        return lax.all_gather(value[0], "ez", axis=0, tiled=False)

    with jax.named_scope("gather_along_z"):
        fwd_tok_z = gather_z(fwd_tokens)
        fwd_routes_z = gather_z(fwd_routes)
        fwd_weights_z = gather_z(fwd_weights)
        bwd_tok_z = gather_z(bwd_tokens)
        bwd_grads_z = gather_z(bwd_grads)
        bwd_routes_z = gather_z(bwd_routes)
        bwd_weights_z = gather_z(bwd_weights)

    with jax.named_scope("slots"):
        fwd_slots = local_slots(
            fwd_routes_z, slot_positions(fwd_routes_z, expert_count), expert_class, class_count, capacity
        )
        bwd_slots = local_slots(
            bwd_routes_z, slot_positions(bwd_routes_z, expert_count), expert_class, class_count, capacity
        )

    with jax.named_scope("forward_experts"):
        (fwd_packed,) = pack_rows((fwd_tok_z,), fwd_slots, slot_total)
        fwd_rows = to_experts(fwd_packed, x_count, capacity)
        fwd_res = forward_work(fwd_rows, w_up, w_down)
        fwd_back = from_experts(fwd_res, z_count, x_count, capacity)
        fwd_part = weighted_partial(fwd_back, fwd_slots, fwd_weights_z)
        fwd_out = sum_back(fwd_tokens[0], fwd_part)

    with jax.named_scope("backward_experts"):
        bwd_packed, grad_packed = pack_rows((bwd_tok_z, bwd_grads_z), bwd_slots, slot_total)
        bwd_rows = to_experts(bwd_packed, x_count, capacity)
        grad_rows = to_experts(grad_packed, x_count, capacity)
        bwd_res = backward_work(bwd_rows, grad_rows, w_up, w_down)
        bwd_back = from_experts(bwd_res, z_count, x_count, capacity)
        bwd_part = weighted_partial(bwd_back, bwd_slots, bwd_weights_z)
        bwd_out = sum_back(bwd_grads[0], bwd_part)

    next_input = from_behind(fwd_out[None], "pp", 1)
    prev_grad = from_behind(bwd_out[None], "pp", -1)
    return (next_input, prev_grad)


def solution(mesh):
    devices = mesh.devices
    pp_count, ep_count = devices.shape
    split_mesh = Mesh(devices.reshape(pp_count, ep_count // Z_PARTS, Z_PARTS), ("pp", "ex", "ez"))
    rows = P("pp", ("ex", "ez"), None)
    placed = (rows, rows, rows, rows, rows, rows, rows, P("pp", None, ("ex", "ez")), rows)
    return jax.shard_map(
        on_device,
        mesh=split_mesh,
        in_specs=placed,
        out_specs=(rows, rows),
        check_vma=False,
    )
```

```python
import jax
import jax.numpy as jnp
from jax import lax
from jax.sharding import Mesh
from jax.sharding import PartitionSpec as P

Z_PARTS = 4


def from_behind(value, axis, by):
    size = lax.axis_size(axis)
    return lax.ppermute(value, axis, [(i, (i + by) % size) for i in range(size)])


def silu_slope(pre_act):
    sigmoid_value = jax.nn.sigmoid(pre_act)
    return sigmoid_value * (1.0 + pre_act * (1.0 - sigmoid_value))


def slot_positions(chosen, expert_count):
    groups, tok_rows, route_count = chosen.shape
    onehot = (chosen[..., None] == jnp.arange(expert_count, dtype=jnp.int32)).astype(jnp.int32)
    flat_hot = onehot.reshape(groups, tok_rows * route_count, expert_count)
    earlier = jnp.cumsum(flat_hot, axis=1) - flat_hot
    return jnp.sum(earlier * flat_hot, axis=2).reshape(groups, tok_rows, route_count)


def local_slots(chosen, position, expert_class, class_count, capacity):
    column = chosen // class_count
    mine = (chosen % class_count) == expert_class
    return jnp.where(mine, column * capacity + position, -1)


def pack_rows(sources, slots, slot_total):
    table = jnp.sum(
        (slots[..., None] == jnp.arange(slot_total, dtype=jnp.int32)).astype(jnp.bfloat16), axis=2
    )
    return tuple(
        jnp.einsum("gts,gtd->gsd", table, member, preferred_element_type=jnp.float32).astype(jnp.bfloat16)
        for member in sources
    )


def weighted_partial(results, slots, route_weights):
    groups, slot_total, features = results.shape
    route_count = slots.shape[2]
    places = jnp.arange(slot_total, dtype=jnp.int32)
    total = None
    for k in range(route_count):
        table = (slots[:, :, k, None] == places).astype(jnp.bfloat16)
        picked = jnp.einsum("gts,gsd->gtd", table, results, preferred_element_type=jnp.float32)
        term = route_weights[:, :, k, None] * picked
        total = term if total is None else total + term
    return total.astype(jnp.bfloat16)


def forward_work(rows, w_up, w_down):
    hidden = jax.nn.silu(jnp.dot(rows, w_up, preferred_element_type=jnp.float32)).astype(jnp.bfloat16)
    return jnp.dot(hidden, w_down, preferred_element_type=jnp.float32).astype(jnp.bfloat16)


def backward_work(rows, grad_rows, w_up, w_down):
    pre_act = jnp.dot(rows, w_up, preferred_element_type=jnp.float32)
    upstream = lax.dot_general(grad_rows, w_down, (((1,), (1,)), ((), ())), preferred_element_type=jnp.float32)
    hidden_grad = (silu_slope(pre_act) * upstream).astype(jnp.bfloat16)
    return lax.dot_general(
        hidden_grad, w_up, (((1,), (1,)), ((), ())), preferred_element_type=jnp.float32
    ).astype(jnp.bfloat16)


def to_experts(packed, x_count, capacity):
    groups, slot_total, features = packed.shape
    spread = packed.reshape(groups, x_count, capacity, features)
    got = lax.all_to_all(spread, "ex", split_axis=1, concat_axis=1, tiled=True)
    return got.reshape(groups * x_count * capacity, features)


def from_experts(rows, groups, x_count, capacity):
    features = rows.shape[-1]
    spread = rows.reshape(groups, x_count, capacity, features)
    back = lax.all_to_all(spread, "ex", split_axis=1, concat_axis=1, tiled=True)
    return back.reshape(groups, x_count * capacity, features)


def sum_back(residual, partial):
    got = lax.all_to_all(partial, "ez", split_axis=0, concat_axis=0, tiled=True)
    total = residual.astype(jnp.float32) + jnp.sum(got.astype(jnp.float32), axis=0)
    return total.astype(jnp.bfloat16)


def on_device(
    fwd_tokens,
    fwd_routes,
    fwd_weights,
    bwd_tokens,
    bwd_grads,
    bwd_routes,
    bwd_weights,
    up_proj,
    down_proj,
):
    x_count = lax.axis_size("ex")
    z_count = lax.axis_size("ez")
    ep_count = x_count * z_count
    expert_count = ep_count // 2
    class_count = expert_count // x_count
    tok_rows = fwd_tokens.shape[1]
    route_count = fwd_routes.shape[2]
    capacity = 3 * tok_rows * route_count // ep_count
    slot_total = x_count * capacity
    z_index = lax.axis_index("ez")
    expert_class = z_index // (z_count // class_count)
    w_up = up_proj[0]
    w_down = down_proj[0]

    def gather_z(value):
        return lax.all_gather(value[0], "ez", axis=0, tiled=False)

    with jax.named_scope("gather_along_z"):
        fwd_tok_z = gather_z(fwd_tokens)
        bwd_tok_z = gather_z(bwd_tokens)
        bwd_grads_z = gather_z(bwd_grads)
        meta = jnp.concatenate(
            [fwd_routes.astype(jnp.float32), fwd_weights, bwd_routes.astype(jnp.float32), bwd_weights], axis=-1
        )
        meta_z = gather_z(meta)
        fwd_routes_z = meta_z[:, :, 0:route_count].astype(jnp.int32)
        fwd_weights_z = meta_z[:, :, route_count : 2 * route_count]
        bwd_routes_z = meta_z[:, :, 2 * route_count : 3 * route_count].astype(jnp.int32)
        bwd_weights_z = meta_z[:, :, 3 * route_count : 4 * route_count]

    with jax.named_scope("slots"):
        fwd_slots = local_slots(
            fwd_routes_z, slot_positions(fwd_routes_z, expert_count), expert_class, class_count, capacity
        )
        bwd_slots = local_slots(
            bwd_routes_z, slot_positions(bwd_routes_z, expert_count), expert_class, class_count, capacity
        )

    with jax.named_scope("forward_experts"):
        (fwd_packed,) = pack_rows((fwd_tok_z,), fwd_slots, slot_total)
        fwd_rows = to_experts(fwd_packed, x_count, capacity)
        fwd_rows, bwd_tok_z = lax.optimization_barrier((fwd_rows, bwd_tok_z))
        fwd_res = forward_work(fwd_rows, w_up, w_down)
        fwd_back = from_experts(fwd_res, z_count, x_count, capacity)
        fwd_back, bwd_grads_z = lax.optimization_barrier((fwd_back, bwd_grads_z))
        fwd_part = weighted_partial(fwd_back, fwd_slots, fwd_weights_z)
        fwd_out = sum_back(fwd_tokens[0], fwd_part)

    with jax.named_scope("backward_experts"):
        bwd_packed, grad_packed = pack_rows((bwd_tok_z, bwd_grads_z), bwd_slots, slot_total)
        bwd_rows = to_experts(bwd_packed, x_count, capacity)
        grad_rows = to_experts(grad_packed, x_count, capacity)
        bwd_res = backward_work(bwd_rows, grad_rows, w_up, w_down)
        bwd_back = from_experts(bwd_res, z_count, x_count, capacity)
        bwd_part = weighted_partial(bwd_back, bwd_slots, bwd_weights_z)
        bwd_out = sum_back(bwd_grads[0], bwd_part)

    next_input = from_behind(fwd_out[None], "pp", 1)
    prev_grad = from_behind(bwd_out[None], "pp", -1)
    return (next_input, prev_grad)


def solution(mesh):
    devices = mesh.devices
    pp_count, ep_count = devices.shape
    split_mesh = Mesh(devices.reshape(pp_count, ep_count // Z_PARTS, Z_PARTS), ("pp", "ex", "ez"))
    rows = P("pp", ("ex", "ez"), None)
    placed = (rows, rows, rows, rows, rows, rows, rows, P("pp", None, ("ex", "ez")), rows)
    return jax.shard_map(
        on_device,
        mesh=split_mesh,
        in_specs=placed,
        out_specs=(rows, rows),
        check_vma=False,
    )
```

```python
import jax
import jax.numpy as jnp
from jax import lax
from jax.sharding import Mesh
from jax.sharding import PartitionSpec as P

Z_PARTS = 4


def from_behind(value, axis, by):
    size = lax.axis_size(axis)
    return lax.ppermute(value, axis, [(i, (i + by) % size) for i in range(size)])


def silu_slope(pre_act):
    sigmoid_value = jax.nn.sigmoid(pre_act)
    return sigmoid_value * (1.0 + pre_act * (1.0 - sigmoid_value))


def slot_positions(chosen, expert_count):
    groups, tok_rows, route_count = chosen.shape
    onehot = (chosen[..., None] == jnp.arange(expert_count, dtype=jnp.int32)).astype(jnp.int32)
    flat_hot = onehot.reshape(groups, tok_rows * route_count, expert_count)
    earlier = jnp.cumsum(flat_hot, axis=1) - flat_hot
    return jnp.sum(earlier * flat_hot, axis=2).reshape(groups, tok_rows, route_count)


def local_slots(chosen, position, expert_class, class_count, capacity):
    column = chosen // class_count
    mine = (chosen % class_count) == expert_class
    return jnp.where(mine, column * capacity + position, -1)


def pack_rows(sources, slots, slot_total):
    table = jnp.sum(
        (slots[..., None] == jnp.arange(slot_total, dtype=jnp.int32)).astype(jnp.bfloat16), axis=2
    )
    return tuple(
        jnp.einsum("gts,gtd->gsd", table, member, preferred_element_type=jnp.float32).astype(jnp.bfloat16)
        for member in sources
    )


def weighted_partial(results, slots, route_weights):
    groups, slot_total, features = results.shape
    route_count = slots.shape[2]
    places = jnp.arange(slot_total, dtype=jnp.int32)
    total = None
    for k in range(route_count):
        table = (slots[:, :, k, None] == places).astype(jnp.bfloat16)
        picked = jnp.einsum("gts,gsd->gtd", table, results, preferred_element_type=jnp.float32)
        term = route_weights[:, :, k, None] * picked
        total = term if total is None else total + term
    return total


def forward_work(rows, w_up, w_down):
    hidden = jax.nn.silu(jnp.dot(rows, w_up, preferred_element_type=jnp.float32)).astype(jnp.bfloat16)
    return jnp.dot(hidden, w_down, preferred_element_type=jnp.float32).astype(jnp.bfloat16)


def backward_work(rows, grad_rows, w_up, w_down):
    pre_act = jnp.dot(rows, w_up, preferred_element_type=jnp.float32)
    upstream = lax.dot_general(grad_rows, w_down, (((1,), (1,)), ((), ())), preferred_element_type=jnp.float32)
    hidden_grad = (silu_slope(pre_act) * upstream).astype(jnp.bfloat16)
    return lax.dot_general(
        hidden_grad, w_up, (((1,), (1,)), ((), ())), preferred_element_type=jnp.float32
    ).astype(jnp.bfloat16)


def to_experts(packed, x_count, capacity):
    groups, slot_total, features = packed.shape
    spread = packed.reshape(groups, x_count, capacity, features)
    got = lax.all_to_all(spread, "ex", split_axis=1, concat_axis=1, tiled=True)
    return got.reshape(groups * x_count * capacity, features)


def from_experts(rows, groups, x_count, capacity):
    features = rows.shape[-1]
    spread = rows.reshape(groups, x_count, capacity, features)
    back = lax.all_to_all(spread, "ex", split_axis=1, concat_axis=1, tiled=True)
    return back.reshape(groups, x_count * capacity, features)


def sum_back(residual, partial, z_index):
    own = (jnp.arange(partial.shape[0]) == z_index)[:, None, None]
    partial = partial + jnp.where(own, residual.astype(jnp.float32)[None], 0.0)
    total = lax.psum_scatter(partial, "ez", scatter_dimension=0, tiled=False)
    return total.astype(jnp.bfloat16)


def on_device(
    fwd_tokens,
    fwd_routes,
    fwd_weights,
    bwd_tokens,
    bwd_grads,
    bwd_routes,
    bwd_weights,
    up_proj,
    down_proj,
):
    x_count = lax.axis_size("ex")
    z_count = lax.axis_size("ez")
    ep_count = x_count * z_count
    expert_count = ep_count // 2
    class_count = expert_count // x_count
    tok_rows = fwd_tokens.shape[1]
    route_count = fwd_routes.shape[2]
    capacity = 3 * tok_rows * route_count // ep_count
    slot_total = x_count * capacity
    z_index = lax.axis_index("ez")
    expert_class = z_index // (z_count // class_count)
    w_up = up_proj[0]
    w_down = down_proj[0]

    def gather_z(value):
        return lax.all_gather(value[0], "ez", axis=0, tiled=False)

    with jax.named_scope("gather_along_z"):
        fwd_tok_z = gather_z(fwd_tokens)
        bwd_tok_z = gather_z(bwd_tokens)
        bwd_grads_z = gather_z(bwd_grads)
        meta = jnp.concatenate(
            [fwd_routes.astype(jnp.float32), fwd_weights, bwd_routes.astype(jnp.float32), bwd_weights], axis=-1
        )
        meta_z = gather_z(meta)
        fwd_routes_z = meta_z[:, :, 0:route_count].astype(jnp.int32)
        fwd_weights_z = meta_z[:, :, route_count : 2 * route_count]
        bwd_routes_z = meta_z[:, :, 2 * route_count : 3 * route_count].astype(jnp.int32)
        bwd_weights_z = meta_z[:, :, 3 * route_count : 4 * route_count]

    with jax.named_scope("slots"):
        fwd_slots = local_slots(
            fwd_routes_z, slot_positions(fwd_routes_z, expert_count), expert_class, class_count, capacity
        )
        bwd_slots = local_slots(
            bwd_routes_z, slot_positions(bwd_routes_z, expert_count), expert_class, class_count, capacity
        )

    with jax.named_scope("forward_experts"):
        (fwd_packed,) = pack_rows((fwd_tok_z,), fwd_slots, slot_total)
        fwd_rows = to_experts(fwd_packed, x_count, capacity)
        fwd_rows, bwd_tok_z = lax.optimization_barrier((fwd_rows, bwd_tok_z))
        fwd_res = forward_work(fwd_rows, w_up, w_down)
        fwd_back = from_experts(fwd_res, z_count, x_count, capacity)
        fwd_back, bwd_grads_z = lax.optimization_barrier((fwd_back, bwd_grads_z))
        fwd_part = weighted_partial(fwd_back, fwd_slots, fwd_weights_z)
        fwd_out = sum_back(fwd_tokens[0], fwd_part, z_index)

    with jax.named_scope("backward_experts"):
        bwd_packed, grad_packed = pack_rows((bwd_tok_z, bwd_grads_z), bwd_slots, slot_total)
        bwd_rows = to_experts(bwd_packed, x_count, capacity)
        grad_rows = to_experts(grad_packed, x_count, capacity)
        bwd_res = backward_work(bwd_rows, grad_rows, w_up, w_down)
        bwd_back = from_experts(bwd_res, z_count, x_count, capacity)
        bwd_part = weighted_partial(bwd_back, bwd_slots, bwd_weights_z)
        bwd_out = sum_back(bwd_grads[0], bwd_part, z_index)

    next_input = from_behind(fwd_out[None], "pp", 1)
    prev_grad = from_behind(bwd_out[None], "pp", -1)
    return (next_input, prev_grad)


def solution(mesh):
    devices = mesh.devices
    pp_count, ep_count = devices.shape
    split_mesh = Mesh(devices.reshape(pp_count, ep_count // Z_PARTS, Z_PARTS), ("pp", "ex", "ez"))
    rows = P("pp", ("ex", "ez"), None)
    placed = (rows, rows, rows, rows, rows, rows, rows, P("pp", None, ("ex", "ez")), rows)
    return jax.shard_map(
        on_device,
        mesh=split_mesh,
        in_specs=placed,
        out_specs=(rows, rows),
        check_vma=False,
    )
```

```python
import jax
import jax.numpy as jnp
from jax import lax
from jax.sharding import Mesh
from jax.sharding import PartitionSpec as P

Z_PARTS = 4


def from_behind(value, axis, by):
    size = lax.axis_size(axis)
    return lax.ppermute(value, axis, [(i, (i + by) % size) for i in range(size)])


def silu_slope(pre_act):
    sigmoid_value = jax.nn.sigmoid(pre_act)
    return sigmoid_value * (1.0 + pre_act * (1.0 - sigmoid_value))


def slot_positions(chosen, expert_count):
    groups, tok_rows, route_count = chosen.shape
    onehot = (chosen[..., None] == jnp.arange(expert_count, dtype=jnp.int32)).astype(jnp.int32)
    flat_hot = onehot.reshape(groups, tok_rows * route_count, expert_count)
    earlier = jnp.cumsum(flat_hot, axis=1) - flat_hot
    return jnp.sum(earlier * flat_hot, axis=2).reshape(groups, tok_rows, route_count)


def local_slots(chosen, position, expert_class, class_count, capacity):
    groups = chosen.shape[0]
    column = chosen // class_count
    mine = (chosen % class_count) == expert_class
    group = jnp.arange(groups, dtype=jnp.int32)[:, None, None]
    return jnp.where(mine, (column * groups + group) * capacity + position, -1)


def slot_table(slots, slot_total):
    flat = slots.reshape(-1, slots.shape[-1])
    return jnp.sum((flat[..., None] == jnp.arange(slot_total, dtype=jnp.int32)).astype(jnp.bfloat16), axis=1)


def pack_rows(member, table):
    flat = member.reshape(-1, member.shape[-1])
    return lax.dot_general(
        table, flat, (((0,), (0,)), ((), ())), preferred_element_type=jnp.float32
    ).astype(jnp.bfloat16)


def weighted_partial(results, slots, route_weights, slot_total):
    groups, tok_rows, route_count = slots.shape
    places = jnp.arange(slot_total, dtype=jnp.int32)
    total = None
    for k in range(route_count):
        table = (slots[:, :, k].reshape(-1, 1) == places).astype(jnp.bfloat16)
        picked = jnp.dot(table, results, preferred_element_type=jnp.float32)
        term = route_weights[:, :, k].reshape(-1, 1) * picked
        total = term if total is None else total + term
    return total.reshape(groups, tok_rows, -1)


def forward_work(rows, w_up, w_down):
    hidden = jax.nn.silu(jnp.dot(rows, w_up, preferred_element_type=jnp.float32)).astype(jnp.bfloat16)
    return jnp.dot(hidden, w_down, preferred_element_type=jnp.float32).astype(jnp.bfloat16)


def backward_work(rows, grad_rows, w_up, w_down):
    pre_act = jnp.dot(rows, w_up, preferred_element_type=jnp.float32)
    upstream = lax.dot_general(grad_rows, w_down, (((1,), (1,)), ((), ())), preferred_element_type=jnp.float32)
    hidden_grad = (silu_slope(pre_act) * upstream).astype(jnp.bfloat16)
    return lax.dot_general(
        hidden_grad, w_up, (((1,), (1,)), ((), ())), preferred_element_type=jnp.float32
    ).astype(jnp.bfloat16)


def swap_x(rows, x_count):
    spread = rows.reshape((x_count, -1) + rows.shape[1:])
    got = lax.all_to_all(spread, "ex", split_axis=0, concat_axis=0, tiled=True)
    return got.reshape(rows.shape)


def sum_back(residual, partial, z_index, wire_type):
    if wire_type == jnp.float32:
        own = (jnp.arange(partial.shape[0]) == z_index)[:, None, None]
        partial = partial + jnp.where(own, residual.astype(jnp.float32)[None], 0.0)
        total = lax.psum_scatter(partial, "ez", scatter_dimension=0, tiled=False)
    else:
        summed = lax.psum_scatter(partial.astype(wire_type), "ez", scatter_dimension=0, tiled=False)
        total = residual.astype(jnp.float32) + summed.astype(jnp.float32)
    return total.astype(jnp.bfloat16)


def on_device(
    fwd_tokens,
    fwd_routes,
    fwd_weights,
    bwd_tokens,
    bwd_grads,
    bwd_routes,
    bwd_weights,
    up_proj,
    down_proj,
):
    x_count = lax.axis_size("ex")
    z_count = lax.axis_size("ez")
    ep_count = x_count * z_count
    expert_count = ep_count // 2
    class_count = expert_count // x_count
    tok_rows = fwd_tokens.shape[1]
    route_count = fwd_routes.shape[2]
    capacity = 3 * tok_rows * route_count // ep_count
    slot_total = x_count * z_count * capacity
    z_index = lax.axis_index("ez")
    expert_class = z_index // (z_count // class_count)
    w_up = up_proj[0]
    w_down = down_proj[0]

    def gather_z(value):
        return lax.all_gather(value[0], "ez", axis=0, tiled=False)

    with jax.named_scope("gather_along_z"):
        fwd_tok_z = gather_z(fwd_tokens)
        bwd_tok_z = gather_z(bwd_tokens)
        bwd_grads_z = gather_z(bwd_grads)
        meta = jnp.concatenate(
            [fwd_routes.astype(jnp.float32), fwd_weights, bwd_routes.astype(jnp.float32), bwd_weights], axis=-1
        )
        meta_z = gather_z(meta)
        fwd_routes_z = meta_z[:, :, 0:route_count].astype(jnp.int32)
        fwd_weights_z = meta_z[:, :, route_count : 2 * route_count]
        bwd_routes_z = meta_z[:, :, 2 * route_count : 3 * route_count].astype(jnp.int32)
        bwd_weights_z = meta_z[:, :, 3 * route_count : 4 * route_count]

    with jax.named_scope("slots"):
        fwd_slots = local_slots(
            fwd_routes_z, slot_positions(fwd_routes_z, expert_count), expert_class, class_count, capacity
        )
        bwd_slots = local_slots(
            bwd_routes_z, slot_positions(bwd_routes_z, expert_count), expert_class, class_count, capacity
        )

    with jax.named_scope("forward_experts"):
        fwd_table = slot_table(fwd_slots, slot_total)
        fwd_rows = swap_x(pack_rows(fwd_tok_z, fwd_table), x_count)
        fwd_rows, bwd_tok_z = lax.optimization_barrier((fwd_rows, bwd_tok_z))
        fwd_res = forward_work(fwd_rows, w_up, w_down)
        fwd_back = swap_x(fwd_res, x_count)
        fwd_back, bwd_grads_z = lax.optimization_barrier((fwd_back, bwd_grads_z))
        fwd_part = weighted_partial(fwd_back, fwd_slots, fwd_weights_z, slot_total)
        fwd_out = sum_back(fwd_tokens[0], fwd_part, z_index, jnp.float32)

    with jax.named_scope("backward_experts"):
        bwd_table = slot_table(bwd_slots, slot_total)
        features = bwd_tok_z.shape[-1]
        both = jnp.stack(
            [
                pack_rows(bwd_tok_z, bwd_table).reshape(x_count, -1, features),
                pack_rows(bwd_grads_z, bwd_table).reshape(x_count, -1, features),
            ],
            axis=1,
        )
        both = swap_x(both, x_count)
        bwd_rows = both[:, 0].reshape(-1, features)
        grad_rows = both[:, 1].reshape(-1, features)
        bwd_res = backward_work(bwd_rows, grad_rows, w_up, w_down)
        bwd_back = swap_x(bwd_res, x_count)
        bwd_part = weighted_partial(bwd_back, bwd_slots, bwd_weights_z, slot_total)
        bwd_out = sum_back(bwd_grads[0], bwd_part, z_index, jnp.bfloat16)

    next_input = from_behind(fwd_out[None], "pp", 1)
    prev_grad = from_behind(bwd_out[None], "pp", -1)
    return (next_input, prev_grad)


def solution(mesh):
    devices = mesh.devices
    pp_count, ep_count = devices.shape
    split_mesh = Mesh(devices.reshape(pp_count, ep_count // Z_PARTS, Z_PARTS), ("pp", "ex", "ez"))
    rows = P("pp", ("ex", "ez"), None)
    placed = (rows, rows, rows, rows, rows, rows, rows, P("pp", None, ("ex", "ez")), rows)
    return jax.shard_map(
        on_device,
        mesh=split_mesh,
        in_specs=placed,
        out_specs=(rows, rows),
        check_vma=False,
    )
```

```python
import jax
import jax.numpy as jnp
from jax import lax
from jax.sharding import Mesh
from jax.sharding import PartitionSpec as P

Z_PARTS = 4
D_PARTS = 2


def from_behind(value, axis, by):
    size = lax.axis_size(axis)
    return lax.ppermute(value, axis, [(i, (i + by) % size) for i in range(size)])


def silu_slope(pre_act):
    sigmoid_value = jax.nn.sigmoid(pre_act)
    return sigmoid_value * (1.0 + pre_act * (1.0 - sigmoid_value))


def slot_positions(chosen, expert_count):
    groups, tok_rows, route_count = chosen.shape
    onehot = (chosen[..., None] == jnp.arange(expert_count, dtype=jnp.int32)).astype(jnp.int32)
    flat_hot = onehot.reshape(groups, tok_rows * route_count, expert_count)
    earlier = jnp.cumsum(flat_hot, axis=1) - flat_hot
    return jnp.sum(earlier * flat_hot, axis=2).reshape(groups, tok_rows, route_count)


def local_slots(chosen, position, expert_class, class_count, capacity):
    groups = chosen.shape[0]
    column = chosen // class_count
    mine = (chosen % class_count) == expert_class
    group = jnp.arange(groups, dtype=jnp.int32)[:, None, None]
    return jnp.where(mine, (column * groups + group) * capacity + position, -1)


def slot_table(slots, slot_total):
    flat = slots.reshape(-1, slots.shape[-1])
    return jnp.sum((flat[..., None] == jnp.arange(slot_total, dtype=jnp.int32)).astype(jnp.bfloat16), axis=1)


def pack_rows(member, table):
    flat = member.reshape(-1, member.shape[-1])
    return lax.dot_general(
        table, flat, (((0,), (0,)), ((), ())), preferred_element_type=jnp.float32
    ).astype(jnp.bfloat16)


def weighted_partial(results, slots, route_weights, slot_total):
    groups, tok_rows, route_count = slots.shape
    places = jnp.arange(slot_total, dtype=jnp.int32)
    total = None
    for k in range(route_count):
        table = (slots[:, :, k].reshape(-1, 1) == places).astype(jnp.bfloat16)
        picked = jnp.dot(table, results, preferred_element_type=jnp.float32)
        term = route_weights[:, :, k].reshape(-1, 1) * picked
        total = term if total is None else total + term
    return total.reshape(groups, tok_rows, -1)


def forward_work(row_parts, w_up_parts, w_down):
    pre_act = None
    for rows, w_up in zip(row_parts, w_up_parts):
        term = jnp.dot(rows, w_up, preferred_element_type=jnp.float32)
        pre_act = term if pre_act is None else pre_act + term
    hidden = jax.nn.silu(pre_act).astype(jnp.bfloat16)
    return jnp.dot(hidden, w_down, preferred_element_type=jnp.float32).astype(jnp.bfloat16)


def backward_work(rows, grad_rows, w_up, w_down, w_up_parts):
    pre_act = jnp.dot(rows, w_up, preferred_element_type=jnp.float32)
    upstream = lax.dot_general(grad_rows, w_down, (((1,), (1,)), ((), ())), preferred_element_type=jnp.float32)
    hidden_grad = (silu_slope(pre_act) * upstream).astype(jnp.bfloat16)
    return [
        lax.dot_general(hidden_grad, part, (((1,), (1,)), ((), ())), preferred_element_type=jnp.float32).astype(
            jnp.bfloat16
        )
        for part in w_up_parts
    ]


def swap_x(rows, x_count):
    spread = rows.reshape((x_count, -1) + rows.shape[1:])
    got = lax.all_to_all(spread, "ex", split_axis=0, concat_axis=0, tiled=True)
    return got.reshape(rows.shape)


def sum_back(residual, partial, z_index, wire_type):
    if wire_type == jnp.float32:
        own = (jnp.arange(partial.shape[0]) == z_index)[:, None, None]
        partial = partial + jnp.where(own, residual.astype(jnp.float32)[None], 0.0)
        total = lax.psum_scatter(partial, "ez", scatter_dimension=0, tiled=False)
    else:
        summed = lax.psum_scatter(partial.astype(wire_type), "ez", scatter_dimension=0, tiled=False)
        total = residual.astype(jnp.float32) + summed.astype(jnp.float32)
    return total.astype(jnp.bfloat16)


def on_device(
    fwd_tokens,
    fwd_routes,
    fwd_weights,
    bwd_tokens,
    bwd_grads,
    bwd_routes,
    bwd_weights,
    up_proj,
    down_proj,
):
    x_count = lax.axis_size("ex")
    z_count = lax.axis_size("ez")
    ep_count = x_count * z_count
    expert_count = ep_count // 2
    class_count = expert_count // x_count
    tok_rows = fwd_tokens.shape[1]
    route_count = fwd_routes.shape[2]
    capacity = 3 * tok_rows * route_count // ep_count
    slot_total = x_count * z_count * capacity
    z_index = lax.axis_index("ez")
    expert_class = z_index // (z_count // class_count)
    w_up = up_proj[0]
    w_down = down_proj[0]

    def gather_z(value):
        return lax.all_gather(value[0], "ez", axis=0, tiled=False)

    features = fwd_tokens.shape[-1]
    cuts = [(i * features // D_PARTS, (i + 1) * features // D_PARTS) for i in range(D_PARTS)]
    w_up_parts = [w_up[lo:hi] for lo, hi in cuts]

    with jax.named_scope("gather_along_z"):
        fwd_tok_parts = [gather_z(fwd_tokens[:, :, lo:hi]) for lo, hi in cuts]
        bwd_tok_z = gather_z(bwd_tokens)
        bwd_grads_z = gather_z(bwd_grads)
        meta = jnp.concatenate(
            [fwd_routes.astype(jnp.float32), fwd_weights, bwd_routes.astype(jnp.float32), bwd_weights], axis=-1
        )
        meta_z = gather_z(meta)
        fwd_routes_z = meta_z[:, :, 0:route_count].astype(jnp.int32)
        fwd_weights_z = meta_z[:, :, route_count : 2 * route_count]
        bwd_routes_z = meta_z[:, :, 2 * route_count : 3 * route_count].astype(jnp.int32)
        bwd_weights_z = meta_z[:, :, 3 * route_count : 4 * route_count]

    with jax.named_scope("slots"):
        fwd_slots = local_slots(
            fwd_routes_z, slot_positions(fwd_routes_z, expert_count), expert_class, class_count, capacity
        )
        bwd_slots = local_slots(
            bwd_routes_z, slot_positions(bwd_routes_z, expert_count), expert_class, class_count, capacity
        )

    with jax.named_scope("forward_experts"):
        fwd_table = slot_table(fwd_slots, slot_total)
        fwd_row_parts = [swap_x(pack_rows(part, fwd_table), x_count) for part in fwd_tok_parts]
        fwd_row_parts, bwd_tok_z = lax.optimization_barrier((fwd_row_parts, bwd_tok_z))
        fwd_res = forward_work(fwd_row_parts, w_up_parts, w_down)
        fwd_back = swap_x(fwd_res, x_count)
        fwd_back, bwd_grads_z = lax.optimization_barrier((fwd_back, bwd_grads_z))
        fwd_part = weighted_partial(fwd_back, fwd_slots, fwd_weights_z, slot_total)

    with jax.named_scope("backward_experts"):
        bwd_table = slot_table(bwd_slots, slot_total)
        both = jnp.stack(
            [
                pack_rows(bwd_tok_z, bwd_table).reshape(x_count, -1, features),
                pack_rows(bwd_grads_z, bwd_table).reshape(x_count, -1, features),
            ],
            axis=1,
        )
        fwd_part, both = lax.optimization_barrier((fwd_part, both))
        both = swap_x(both, x_count)
        bwd_rows = both[:, 0].reshape(-1, features)
        grad_rows = both[:, 1].reshape(-1, features)
        fwd_out = sum_back(fwd_tokens[0], fwd_part, z_index, jnp.float32)
        bwd_res_parts = backward_work(bwd_rows, grad_rows, w_up, w_down, w_up_parts)
        fwd_out, bwd_res_parts = lax.optimization_barrier((fwd_out, bwd_res_parts))
        next_input = from_behind(fwd_out[None], "pp", 1)
        prev_parts = []
        for (lo, hi), bwd_res in zip(cuts, bwd_res_parts):
            bwd_back = swap_x(bwd_res, x_count)
            bwd_part = weighted_partial(bwd_back, bwd_slots, bwd_weights_z, slot_total)
            bwd_out = sum_back(bwd_grads[0][:, lo:hi], bwd_part, z_index, jnp.bfloat16)
            prev_parts.append(from_behind(bwd_out[None], "pp", -1))
        prev_grad = jnp.concatenate(prev_parts, axis=-1)

    return (next_input, prev_grad)


def solution(mesh):
    devices = mesh.devices
    pp_count, ep_count = devices.shape
    split_mesh = Mesh(devices.reshape(pp_count, ep_count // Z_PARTS, Z_PARTS), ("pp", "ex", "ez"))
    rows = P("pp", ("ex", "ez"), None)
    placed = (rows, rows, rows, rows, rows, rows, rows, P("pp", None, ("ex", "ez")), rows)
    return jax.shard_map(
        on_device,
        mesh=split_mesh,
        in_specs=placed,
        out_specs=(rows, rows),
        check_vma=False,
    )
```

```python
import jax
import jax.numpy as jnp
from jax import lax
from jax.sharding import Mesh
from jax.sharding import PartitionSpec as P

Z_PARTS = 4
D_PARTS = 2


def from_behind(value, axis, by):
    size = lax.axis_size(axis)
    return lax.ppermute(value, axis, [(i, (i + by) % size) for i in range(size)])


def silu_slope(pre_act):
    sigmoid_value = jax.nn.sigmoid(pre_act)
    return sigmoid_value * (1.0 + pre_act * (1.0 - sigmoid_value))


def slot_positions(chosen, expert_count):
    groups, tok_rows, route_count = chosen.shape
    onehot = (chosen[..., None] == jnp.arange(expert_count, dtype=jnp.int32)).astype(jnp.int32)
    flat_hot = onehot.reshape(groups, tok_rows * route_count, expert_count)
    earlier = jnp.cumsum(flat_hot, axis=1) - flat_hot
    return jnp.sum(earlier * flat_hot, axis=2).reshape(groups, tok_rows, route_count)


def local_slots(chosen, position, expert_class, class_count, capacity):
    groups = chosen.shape[0]
    column = chosen // class_count
    mine = (chosen % class_count) == expert_class
    group = jnp.arange(groups, dtype=jnp.int32)[:, None, None]
    return jnp.where(mine, (column * groups + group) * capacity + position, -1)


def slot_table(slots, slot_total):
    flat = slots.reshape(-1, slots.shape[-1])
    return jnp.sum((flat[..., None] == jnp.arange(slot_total, dtype=jnp.int32)).astype(jnp.bfloat16), axis=1)


def pack_rows(member, table):
    flat = member.reshape(-1, member.shape[-1])
    return lax.dot_general(
        table, flat, (((0,), (0,)), ((), ())), preferred_element_type=jnp.float32
    ).astype(jnp.bfloat16)


def weighted_partial(results, slots, route_weights, slot_total):
    groups, tok_rows, route_count = slots.shape
    places = jnp.arange(slot_total, dtype=jnp.int32)
    total = None
    for k in range(route_count):
        table = (slots[:, :, k].reshape(-1, 1) == places).astype(jnp.bfloat16)
        picked = jnp.dot(table, results, preferred_element_type=jnp.float32)
        term = route_weights[:, :, k].reshape(-1, 1) * picked
        total = term if total is None else total + term
    return total.reshape(groups, tok_rows, -1)


def forward_work(rows, w_up, w_down_parts):
    hidden = jax.nn.silu(jnp.dot(rows, w_up, preferred_element_type=jnp.float32)).astype(jnp.bfloat16)
    return [jnp.dot(hidden, part, preferred_element_type=jnp.float32).astype(jnp.bfloat16) for part in w_down_parts]


def backward_work(rows, grad_rows, w_up, w_down):
    pre_act = jnp.dot(rows, w_up, preferred_element_type=jnp.float32)
    upstream = lax.dot_general(grad_rows, w_down, (((1,), (1,)), ((), ())), preferred_element_type=jnp.float32)
    hidden_grad = (silu_slope(pre_act) * upstream).astype(jnp.bfloat16)
    return lax.dot_general(
        hidden_grad, w_up, (((1,), (1,)), ((), ())), preferred_element_type=jnp.float32
    ).astype(jnp.bfloat16)


def swap_x(rows, x_count):
    spread = rows.reshape((x_count, -1) + rows.shape[1:])
    got = lax.all_to_all(spread, "ex", split_axis=0, concat_axis=0, tiled=True)
    return got.reshape(rows.shape)


def sum_back(residual, partial, z_index, wire_type):
    if wire_type == jnp.float32:
        own = (jnp.arange(partial.shape[0]) == z_index)[:, None, None]
        partial = partial + jnp.where(own, residual.astype(jnp.float32)[None], 0.0)
        total = lax.psum_scatter(partial, "ez", scatter_dimension=0, tiled=False)
    else:
        summed = lax.psum_scatter(partial.astype(wire_type), "ez", scatter_dimension=0, tiled=False)
        total = residual.astype(jnp.float32) + summed.astype(jnp.float32)
    return total.astype(jnp.bfloat16)


def on_device(
    fwd_tokens,
    fwd_routes,
    fwd_weights,
    bwd_tokens,
    bwd_grads,
    bwd_routes,
    bwd_weights,
    up_proj,
    down_proj,
):
    x_count = lax.axis_size("ex")
    z_count = lax.axis_size("ez")
    ep_count = x_count * z_count
    expert_count = ep_count // 2
    class_count = expert_count // x_count
    tok_rows = fwd_tokens.shape[1]
    route_count = fwd_routes.shape[2]
    capacity = 3 * tok_rows * route_count // ep_count
    slot_total = x_count * z_count * capacity
    z_index = lax.axis_index("ez")
    expert_class = z_index // (z_count // class_count)
    w_up = up_proj[0]
    w_down = down_proj[0]

    def gather_z(value):
        return lax.all_gather(value[0], "ez", axis=0, tiled=False)

    features = fwd_tokens.shape[-1]
    cuts = [(i * features // D_PARTS, (i + 1) * features // D_PARTS) for i in range(D_PARTS)]

    with jax.named_scope("gather_along_z"):
        bwd_tok_z = gather_z(bwd_tokens)
        bwd_grads_z = gather_z(bwd_grads)
        fwd_tokens_in, bwd_grads_z = lax.optimization_barrier((fwd_tokens, bwd_grads_z))
        fwd_tok_z = gather_z(fwd_tokens_in)
        meta = jnp.concatenate(
            [fwd_routes.astype(jnp.float32), fwd_weights, bwd_routes.astype(jnp.float32), bwd_weights], axis=-1
        )
        meta_z = gather_z(meta)
        fwd_routes_z = meta_z[:, :, 0:route_count].astype(jnp.int32)
        fwd_weights_z = meta_z[:, :, route_count : 2 * route_count]
        bwd_routes_z = meta_z[:, :, 2 * route_count : 3 * route_count].astype(jnp.int32)
        bwd_weights_z = meta_z[:, :, 3 * route_count : 4 * route_count]

    with jax.named_scope("slots"):
        fwd_slots = local_slots(
            fwd_routes_z, slot_positions(fwd_routes_z, expert_count), expert_class, class_count, capacity
        )
        bwd_slots = local_slots(
            bwd_routes_z, slot_positions(bwd_routes_z, expert_count), expert_class, class_count, capacity
        )

    with jax.named_scope("backward_experts"):
        bwd_table = slot_table(bwd_slots, slot_total)
        bwd_rows = swap_x(pack_rows(bwd_tok_z, bwd_table), x_count)
        grad_rows = swap_x(pack_rows(bwd_grads_z, bwd_table), x_count)
        bwd_res = backward_work(bwd_rows, grad_rows, w_up, w_down)

    with jax.named_scope("forward_experts"):
        fwd_table = slot_table(fwd_slots, slot_total)
        fwd_rows = swap_x(pack_rows(fwd_tok_z, fwd_table), x_count)
        fwd_rows, bwd_res = lax.optimization_barrier((fwd_rows, bwd_res))

    with jax.named_scope("backward_experts"):
        bwd_back = swap_x(bwd_res, x_count)
        bwd_part = weighted_partial(bwd_back, bwd_slots, bwd_weights_z, slot_total)
        bwd_out = sum_back(bwd_grads[0], bwd_part, z_index, jnp.bfloat16)
        prev_grad = from_behind(bwd_out[None], "pp", -1)

    with jax.named_scope("forward_experts"):
        w_down_parts = [w_down[:, lo:hi] for lo, hi in cuts]
        fwd_res_parts = forward_work(fwd_rows, w_up, w_down_parts)
        next_parts = []
        for (lo, hi), fwd_res in zip(cuts, fwd_res_parts):
            fwd_back = swap_x(fwd_res, x_count)
            fwd_part = weighted_partial(fwd_back, fwd_slots, fwd_weights_z, slot_total)
            fwd_out = sum_back(fwd_tokens[0][:, lo:hi], fwd_part, z_index, jnp.bfloat16)
            next_parts.append(from_behind(fwd_out[None], "pp", 1))
        next_input = jnp.concatenate(next_parts, axis=-1)

    return (next_input, prev_grad)


def solution(mesh):
    devices = mesh.devices
    pp_count, ep_count = devices.shape
    split_mesh = Mesh(devices.reshape(pp_count, ep_count // Z_PARTS, Z_PARTS), ("pp", "ex", "ez"))
    rows = P("pp", ("ex", "ez"), None)
    placed = (rows, rows, rows, rows, rows, rows, rows, P("pp", None, ("ex", "ez")), rows)
    return jax.shard_map(
        on_device,
        mesh=split_mesh,
        in_specs=placed,
        out_specs=(rows, rows),
        check_vma=False,
    )
```

```python
import jax
import jax.numpy as jnp
from jax import lax
from jax.sharding import Mesh
from jax.sharding import PartitionSpec as P

Z_PARTS = 4
D_PARTS = 2


def from_behind(value, axis, by):
    size = lax.axis_size(axis)
    return lax.ppermute(value, axis, [(i, (i + by) % size) for i in range(size)])


def silu_slope(pre_act):
    sigmoid_value = jax.nn.sigmoid(pre_act)
    return sigmoid_value * (1.0 + pre_act * (1.0 - sigmoid_value))


def slot_positions(chosen, expert_count):
    groups, tok_rows, route_count = chosen.shape
    onehot = (chosen[..., None] == jnp.arange(expert_count, dtype=jnp.int32)).astype(jnp.int32)
    flat_hot = onehot.reshape(groups, tok_rows * route_count, expert_count)
    earlier = jnp.cumsum(flat_hot, axis=1) - flat_hot
    return jnp.sum(earlier * flat_hot, axis=2).reshape(groups, tok_rows, route_count)


def local_slots(chosen, position, expert_class, class_count, capacity):
    groups = chosen.shape[0]
    column = chosen // class_count
    mine = (chosen % class_count) == expert_class
    group = jnp.arange(groups, dtype=jnp.int32)[:, None, None]
    return jnp.where(mine, (column * groups + group) * capacity + position, -1)


def slot_table(slots, slot_total):
    flat = slots.reshape(-1, slots.shape[-1])
    return jnp.sum((flat[..., None] == jnp.arange(slot_total, dtype=jnp.int32)).astype(jnp.bfloat16), axis=1)


def pack_rows(member, table):
    flat = member.reshape(-1, member.shape[-1])
    return lax.dot_general(
        table, flat, (((0,), (0,)), ((), ())), preferred_element_type=jnp.float32
    ).astype(jnp.bfloat16)


def weighted_partial(results, slots, route_weights, slot_total):
    groups, tok_rows, route_count = slots.shape
    places = jnp.arange(slot_total, dtype=jnp.int32)
    total = None
    for k in range(route_count):
        table = (slots[:, :, k].reshape(-1, 1) == places).astype(jnp.bfloat16)
        picked = jnp.dot(table, results, preferred_element_type=jnp.float32)
        term = route_weights[:, :, k].reshape(-1, 1) * picked
        total = term if total is None else total + term
    return total.reshape(groups, tok_rows, -1)


def forward_work(rows, w_up, w_down_parts):
    hidden = jax.nn.silu(jnp.dot(rows, w_up, preferred_element_type=jnp.float32)).astype(jnp.bfloat16)
    return [jnp.dot(hidden, part, preferred_element_type=jnp.float32).astype(jnp.bfloat16) for part in w_down_parts]


def backward_work(rows, grad_rows, w_up, w_down):
    pre_act = jnp.dot(rows, w_up, preferred_element_type=jnp.float32)
    upstream = lax.dot_general(grad_rows, w_down, (((1,), (1,)), ((), ())), preferred_element_type=jnp.float32)
    hidden_grad = (silu_slope(pre_act) * upstream).astype(jnp.bfloat16)
    return lax.dot_general(
        hidden_grad, w_up, (((1,), (1,)), ((), ())), preferred_element_type=jnp.float32
    ).astype(jnp.bfloat16)


def swap_x(rows, x_count):
    spread = rows.reshape((x_count, -1) + rows.shape[1:])
    got = lax.all_to_all(spread, "ex", split_axis=0, concat_axis=0, tiled=True)
    return got.reshape(rows.shape)


def sum_back(residual, partial, z_index, wire_type):
    if wire_type == jnp.float32:
        own = (jnp.arange(partial.shape[0]) == z_index)[:, None, None]
        partial = partial + jnp.where(own, residual.astype(jnp.float32)[None], 0.0)
        total = lax.psum_scatter(partial, "ez", scatter_dimension=0, tiled=False)
    else:
        summed = lax.psum_scatter(partial.astype(wire_type), "ez", scatter_dimension=0, tiled=False)
        total = residual.astype(jnp.float32) + summed.astype(jnp.float32)
    return total.astype(jnp.bfloat16)


def on_device(
    fwd_tokens,
    fwd_routes,
    fwd_weights,
    bwd_tokens,
    bwd_grads,
    bwd_routes,
    bwd_weights,
    up_proj,
    down_proj,
):
    x_count = lax.axis_size("ex")
    z_count = lax.axis_size("ez")
    ep_count = x_count * z_count
    expert_count = ep_count // 2
    class_count = expert_count // x_count
    tok_rows = fwd_tokens.shape[1]
    route_count = fwd_routes.shape[2]
    capacity = 3 * tok_rows * route_count // ep_count
    slot_total = x_count * z_count * capacity
    z_index = lax.axis_index("ez")
    expert_class = z_index // (z_count // class_count)
    w_up = up_proj[0]
    w_down = down_proj[0]

    def gather_z(value):
        return lax.all_gather(value[0], "ez", axis=0, tiled=False)

    features = fwd_tokens.shape[-1]
    cuts = [(i * features // D_PARTS, (i + 1) * features // D_PARTS) for i in range(D_PARTS)]

    with jax.named_scope("gather_along_z"):
        bwd_tok_z = gather_z(bwd_tokens)
        bwd_grads_z = gather_z(bwd_grads)
        fwd_tokens_in, bwd_grads_z = lax.optimization_barrier((fwd_tokens, bwd_grads_z))
        fwd_tok_z = gather_z(fwd_tokens_in)
        meta = jnp.concatenate(
            [fwd_routes.astype(jnp.float32), fwd_weights, bwd_routes.astype(jnp.float32), bwd_weights], axis=-1
        )
        meta_z = gather_z(meta)
        fwd_routes_z = meta_z[:, :, 0:route_count].astype(jnp.int32)
        fwd_weights_z = meta_z[:, :, route_count : 2 * route_count]
        bwd_routes_z = meta_z[:, :, 2 * route_count : 3 * route_count].astype(jnp.int32)
        bwd_weights_z = meta_z[:, :, 3 * route_count : 4 * route_count]

    with jax.named_scope("slots"):
        fwd_slots = local_slots(
            fwd_routes_z, slot_positions(fwd_routes_z, expert_count), expert_class, class_count, capacity
        )
        bwd_slots = local_slots(
            bwd_routes_z, slot_positions(bwd_routes_z, expert_count), expert_class, class_count, capacity
        )

    with jax.named_scope("backward_experts"):
        bwd_table = slot_table(bwd_slots, slot_total)
        bwd_rows = swap_x(pack_rows(bwd_tok_z, bwd_table), x_count)
        grad_rows = swap_x(pack_rows(bwd_grads_z, bwd_table), x_count)
        bwd_res = backward_work(bwd_rows, grad_rows, w_up, w_down)

    with jax.named_scope("forward_experts"):
        fwd_table = slot_table(fwd_slots, slot_total)
        fwd_rows = swap_x(pack_rows(fwd_tok_z, fwd_table), x_count)
        fwd_rows, bwd_res = lax.optimization_barrier((fwd_rows, bwd_res))

    with jax.named_scope("forward_experts"):
        w_down_parts = [w_down[:, lo:hi] for lo, hi in cuts]
        fwd_res_parts = forward_work(fwd_rows, w_up, w_down_parts)

    with jax.named_scope("backward_experts"):
        bwd_back = swap_x(bwd_res, x_count)
        bwd_part = weighted_partial(bwd_back, bwd_slots, bwd_weights_z, slot_total)
        bwd_part, fwd_res_parts = lax.optimization_barrier((bwd_part, fwd_res_parts))
        bwd_out = sum_back(bwd_grads[0], bwd_part, z_index, jnp.bfloat16)

    with jax.named_scope("forward_experts"):
        next_parts = []
        for (lo, hi), fwd_res in zip(cuts, fwd_res_parts):
            fwd_back = swap_x(fwd_res, x_count)
            fwd_part = weighted_partial(fwd_back, fwd_slots, fwd_weights_z, slot_total)
            if not next_parts:
                bwd_out, fwd_part = lax.optimization_barrier((bwd_out, fwd_part))
                prev_grad = from_behind(bwd_out[None], "pp", -1)
            fwd_out = sum_back(fwd_tokens[0][:, lo:hi], fwd_part, z_index, jnp.bfloat16)
            next_parts.append(from_behind(fwd_out[None], "pp", 1))
        next_input = jnp.concatenate(next_parts, axis=-1)

    return (next_input, prev_grad)


def solution(mesh):
    devices = mesh.devices
    pp_count, ep_count = devices.shape
    split_mesh = Mesh(devices.reshape(pp_count, ep_count // Z_PARTS, Z_PARTS), ("pp", "ex", "ez"))
    rows = P("pp", ("ex", "ez"), None)
    placed = (rows, rows, rows, rows, rows, rows, rows, P("pp", None, ("ex", "ez")), rows)
    return jax.shard_map(
        on_device,
        mesh=split_mesh,
        in_specs=placed,
        out_specs=(rows, rows),
        check_vma=False,
    )
```

```python
import jax
import jax.numpy as jnp
from jax import lax
from jax.sharding import Mesh
from jax.sharding import PartitionSpec as P

Z_PARTS = 4
D_PARTS = 2


def from_behind(value, axis, by):
    size = lax.axis_size(axis)
    return lax.ppermute(value, axis, [(i, (i + by) % size) for i in range(size)])


def silu_slope(pre_act):
    sigmoid_value = jax.nn.sigmoid(pre_act)
    return sigmoid_value * (1.0 + pre_act * (1.0 - sigmoid_value))


def slot_positions(chosen, expert_count):
    groups, tok_rows, route_count = chosen.shape
    onehot = (chosen[..., None] == jnp.arange(expert_count, dtype=jnp.int32)).astype(jnp.int32)
    flat_hot = onehot.reshape(groups, tok_rows * route_count, expert_count)
    earlier = jnp.cumsum(flat_hot, axis=1) - flat_hot
    return jnp.sum(earlier * flat_hot, axis=2).reshape(groups, tok_rows, route_count)


def local_slots(chosen, position, expert_class, class_count, capacity):
    groups = chosen.shape[0]
    column = chosen // class_count
    mine = (chosen % class_count) == expert_class
    group = jnp.arange(groups, dtype=jnp.int32)[:, None, None]
    return jnp.where(mine, (column * groups + group) * capacity + position, -1)


def slot_table(slots, slot_total):
    flat = slots.reshape(-1, slots.shape[-1])
    return jnp.sum((flat[..., None] == jnp.arange(slot_total, dtype=jnp.int32)).astype(jnp.bfloat16), axis=1)


def pack_rows(member, table):
    flat = member.reshape(-1, member.shape[-1])
    return lax.dot_general(
        table, flat, (((0,), (0,)), ((), ())), preferred_element_type=jnp.float32
    ).astype(jnp.bfloat16)


def weighted_partial(results, slots, route_weights, slot_total):
    groups, tok_rows, route_count = slots.shape
    places = jnp.arange(slot_total, dtype=jnp.int32)
    total = None
    for k in range(route_count):
        table = (slots[:, :, k].reshape(-1, 1) == places).astype(jnp.bfloat16)
        picked = jnp.dot(table, results, preferred_element_type=jnp.float32)
        term = route_weights[:, :, k].reshape(-1, 1) * picked
        total = term if total is None else total + term
    return total.reshape(groups, tok_rows, -1)


def forward_work(rows, w_up, w_down_parts):
    hidden = jax.nn.silu(jnp.dot(rows, w_up, preferred_element_type=jnp.float32)).astype(jnp.bfloat16)
    return [jnp.dot(hidden, part, preferred_element_type=jnp.float32).astype(jnp.bfloat16) for part in w_down_parts]


def backward_work(rows, grad_rows, w_up, w_down):
    pre_act = jnp.dot(rows, w_up, preferred_element_type=jnp.float32)
    upstream = lax.dot_general(grad_rows, w_down, (((1,), (1,)), ((), ())), preferred_element_type=jnp.float32)
    hidden_grad = (silu_slope(pre_act) * upstream).astype(jnp.bfloat16)
    return lax.dot_general(
        hidden_grad, w_up, (((1,), (1,)), ((), ())), preferred_element_type=jnp.float32
    ).astype(jnp.bfloat16)


def swap_x(rows, x_count):
    spread = rows.reshape((x_count, -1) + rows.shape[1:])
    got = lax.all_to_all(spread, "ex", split_axis=0, concat_axis=0, tiled=True)
    return got.reshape(rows.shape)


def sum_back(residual, partial, z_index, wire_type):
    if wire_type == jnp.float32:
        own = (jnp.arange(partial.shape[0]) == z_index)[:, None, None]
        partial = partial + jnp.where(own, residual.astype(jnp.float32)[None], 0.0)
        total = lax.psum_scatter(partial, "ez", scatter_dimension=0, tiled=False)
    else:
        summed = lax.psum_scatter(partial.astype(wire_type), "ez", scatter_dimension=0, tiled=False)
        total = residual.astype(jnp.float32) + summed.astype(jnp.float32)
    return total.astype(jnp.bfloat16)


def swap_sum_back(residual, partial):
    got = lax.all_to_all(partial.astype(jnp.bfloat16), "ez", split_axis=0, concat_axis=0, tiled=True)
    total = residual.astype(jnp.float32) + jnp.sum(got.astype(jnp.float32), axis=0)
    return total.astype(jnp.bfloat16)


def on_device(
    fwd_tokens,
    fwd_routes,
    fwd_weights,
    bwd_tokens,
    bwd_grads,
    bwd_routes,
    bwd_weights,
    up_proj,
    down_proj,
):
    x_count = lax.axis_size("ex")
    z_count = lax.axis_size("ez")
    ep_count = x_count * z_count
    expert_count = ep_count // 2
    class_count = expert_count // x_count
    tok_rows = fwd_tokens.shape[1]
    route_count = fwd_routes.shape[2]
    capacity = 3 * tok_rows * route_count // ep_count
    slot_total = x_count * z_count * capacity
    z_index = lax.axis_index("ez")
    expert_class = z_index // (z_count // class_count)
    w_up = up_proj[0]
    w_down = down_proj[0]

    def gather_z(value):
        return lax.all_gather(value[0], "ez", axis=0, tiled=False)

    features = fwd_tokens.shape[-1]
    cuts = [(i * features // D_PARTS, (i + 1) * features // D_PARTS) for i in range(D_PARTS)]

    with jax.named_scope("gather_along_z"):
        bwd_tok_z = gather_z(bwd_tokens)
        bwd_grads_z = gather_z(bwd_grads)
        fwd_tok_z = gather_z(fwd_tokens)
        meta = jnp.concatenate(
            [fwd_routes.astype(jnp.float32), fwd_weights, bwd_routes.astype(jnp.float32), bwd_weights], axis=-1
        )
        meta_z = gather_z(meta)
        fwd_routes_z = meta_z[:, :, 0:route_count].astype(jnp.int32)
        fwd_weights_z = meta_z[:, :, route_count : 2 * route_count]
        bwd_routes_z = meta_z[:, :, 2 * route_count : 3 * route_count].astype(jnp.int32)
        bwd_weights_z = meta_z[:, :, 3 * route_count : 4 * route_count]

    with jax.named_scope("slots"):
        fwd_slots = local_slots(
            fwd_routes_z, slot_positions(fwd_routes_z, expert_count), expert_class, class_count, capacity
        )
        bwd_slots = local_slots(
            bwd_routes_z, slot_positions(bwd_routes_z, expert_count), expert_class, class_count, capacity
        )

    with jax.named_scope("backward_experts"):
        bwd_table = slot_table(bwd_slots, slot_total)
        bwd_rows = swap_x(pack_rows(bwd_tok_z, bwd_table), x_count)

    with jax.named_scope("dispatch"):
        fwd_table = slot_table(fwd_slots, slot_total)
        pair = jnp.stack(
            [
                pack_rows(bwd_grads_z, bwd_table).reshape(x_count, -1, features),
                pack_rows(fwd_tok_z, fwd_table).reshape(x_count, -1, features),
            ],
            axis=1,
        )
        pair = swap_x(pair, x_count)
        grad_rows = pair[:, 0].reshape(-1, features)
        fwd_rows = pair[:, 1].reshape(-1, features)

    with jax.named_scope("experts"):
        bwd_res = backward_work(bwd_rows, grad_rows, w_up, w_down)
        fwd_res = forward_work(fwd_rows, w_up, [w_down])[0]
        back = jnp.stack(
            [bwd_res.reshape(x_count, -1, features), fwd_res.reshape(x_count, -1, features)], axis=1
        )
        back = swap_x(back, x_count)
        bwd_back = back[:, 0].reshape(-1, features)
        fwd_back = back[:, 1].reshape(-1, features)

    with jax.named_scope("backward_experts"):
        bwd_part = weighted_partial(bwd_back, bwd_slots, bwd_weights_z, slot_total)
        bwd_out = sum_back(bwd_grads[0], bwd_part, z_index, jnp.bfloat16)
        prev_grad = from_behind(bwd_out[None], "pp", -1)

    with jax.named_scope("forward_experts"):
        fwd_part = weighted_partial(fwd_back, fwd_slots, fwd_weights_z, slot_total)
        fwd_out = swap_sum_back(fwd_tokens[0], fwd_part)
        next_input = from_behind(fwd_out[None], "pp", 1)

    return (next_input, prev_grad)


def solution(mesh):
    devices = mesh.devices
    pp_count, ep_count = devices.shape
    split_mesh = Mesh(devices.reshape(pp_count, ep_count // Z_PARTS, Z_PARTS), ("pp", "ex", "ez"))
    rows = P("pp", ("ex", "ez"), None)
    placed = (rows, rows, rows, rows, rows, rows, rows, P("pp", None, ("ex", "ez")), rows)
    return jax.shard_map(
        on_device,
        mesh=split_mesh,
        in_specs=placed,
        out_specs=(rows, rows),
        check_vma=False,
    )
```

```python
import jax
import jax.numpy as jnp
from jax import lax
from jax.sharding import Mesh
from jax.sharding import PartitionSpec as P

Z_PARTS = 4
D_PARTS = 1


def from_behind(value, axis, by):
    size = lax.axis_size(axis)
    return lax.ppermute(value, axis, [(i, (i + by) % size) for i in range(size)])


def silu_slope(pre_act):
    sigmoid_value = jax.nn.sigmoid(pre_act)
    return sigmoid_value * (1.0 + pre_act * (1.0 - sigmoid_value))


def slot_positions(chosen, expert_count):
    groups, tok_rows, route_count = chosen.shape
    onehot = (chosen[..., None] == jnp.arange(expert_count, dtype=jnp.int32)).astype(jnp.int32)
    flat_hot = onehot.reshape(groups, tok_rows * route_count, expert_count)
    earlier = jnp.cumsum(flat_hot, axis=1) - flat_hot
    return jnp.sum(earlier * flat_hot, axis=2).reshape(groups, tok_rows, route_count)


def local_slots(chosen, position, expert_class, class_count, capacity):
    groups = chosen.shape[0]
    column = chosen // class_count
    mine = (chosen % class_count) == expert_class
    group = jnp.arange(groups, dtype=jnp.int32)[:, None, None]
    return jnp.where(mine, (column * groups + group) * capacity + position, -1)


def slot_table(slots, slot_total):
    flat = slots.reshape(-1, slots.shape[-1])
    return jnp.sum((flat[..., None] == jnp.arange(slot_total, dtype=jnp.int32)).astype(jnp.bfloat16), axis=1)


def pack_rows(member, table):
    flat = member.reshape(-1, member.shape[-1])
    return lax.dot_general(
        table, flat, (((0,), (0,)), ((), ())), preferred_element_type=jnp.float32
    ).astype(jnp.bfloat16)


def weighted_partial(results, slots, route_weights, slot_total):
    groups, tok_rows, route_count = slots.shape
    places = jnp.arange(slot_total, dtype=jnp.int32)
    total = None
    for k in range(route_count):
        table = (slots[:, :, k].reshape(-1, 1) == places).astype(jnp.bfloat16)
        picked = jnp.dot(table, results, preferred_element_type=jnp.float32)
        term = route_weights[:, :, k].reshape(-1, 1) * picked
        total = term if total is None else total + term
    return total.reshape(groups, tok_rows, -1)


def forward_work(rows, w_up, w_down_parts):
    hidden = jax.nn.silu(jnp.dot(rows, w_up, preferred_element_type=jnp.float32)).astype(jnp.bfloat16)
    return [jnp.dot(hidden, part, preferred_element_type=jnp.float32).astype(jnp.bfloat16) for part in w_down_parts]


def backward_work(rows, grad_rows, w_up, w_down):
    pre_act = jnp.dot(rows, w_up, preferred_element_type=jnp.float32)
    upstream = lax.dot_general(grad_rows, w_down, (((1,), (1,)), ((), ())), preferred_element_type=jnp.float32)
    hidden_grad = (silu_slope(pre_act) * upstream).astype(jnp.bfloat16)
    return lax.dot_general(
        hidden_grad, w_up, (((1,), (1,)), ((), ())), preferred_element_type=jnp.float32
    ).astype(jnp.bfloat16)


def swap_x(rows, x_count):
    spread = rows.reshape((x_count, -1) + rows.shape[1:])
    got = lax.all_to_all(spread, "ex", split_axis=0, concat_axis=0, tiled=True)
    return got.reshape(rows.shape)


def sum_back(residual, partial, z_index, wire_type):
    if wire_type == jnp.float32:
        own = (jnp.arange(partial.shape[0]) == z_index)[:, None, None]
        partial = partial + jnp.where(own, residual.astype(jnp.float32)[None], 0.0)
        total = lax.psum_scatter(partial, "ez", scatter_dimension=0, tiled=False)
    else:
        summed = lax.psum_scatter(partial.astype(wire_type), "ez", scatter_dimension=0, tiled=False)
        total = residual.astype(jnp.float32) + summed.astype(jnp.float32)
    return total.astype(jnp.bfloat16)


def on_device(
    fwd_tokens,
    fwd_routes,
    fwd_weights,
    bwd_tokens,
    bwd_grads,
    bwd_routes,
    bwd_weights,
    up_proj,
    down_proj,
):
    x_count = lax.axis_size("ex")
    z_count = lax.axis_size("ez")
    ep_count = x_count * z_count
    expert_count = ep_count // 2
    class_count = expert_count // x_count
    tok_rows = fwd_tokens.shape[1]
    route_count = fwd_routes.shape[2]
    capacity = 3 * tok_rows * route_count // ep_count
    slot_total = x_count * z_count * capacity
    z_index = lax.axis_index("ez")
    expert_class = z_index // (z_count // class_count)
    w_up = up_proj[0]
    w_down = down_proj[0]

    def gather_z(value):
        return lax.all_gather(value[0], "ez", axis=0, tiled=False)

    features = fwd_tokens.shape[-1]
    cuts = [(i * features // D_PARTS, (i + 1) * features // D_PARTS) for i in range(D_PARTS)]

    with jax.named_scope("gather_along_z"):
        bwd_tok_z = gather_z(bwd_tokens)
        bwd_grads_z = gather_z(bwd_grads)
        fwd_tokens_in, bwd_grads_z = lax.optimization_barrier((fwd_tokens, bwd_grads_z))
        fwd_tok_z = gather_z(fwd_tokens_in)
        meta = jnp.concatenate(
            [fwd_routes.astype(jnp.float32), fwd_weights, bwd_routes.astype(jnp.float32), bwd_weights], axis=-1
        )
        meta_z = gather_z(meta)
        fwd_routes_z = meta_z[:, :, 0:route_count].astype(jnp.int32)
        fwd_weights_z = meta_z[:, :, route_count : 2 * route_count]
        bwd_routes_z = meta_z[:, :, 2 * route_count : 3 * route_count].astype(jnp.int32)
        bwd_weights_z = meta_z[:, :, 3 * route_count : 4 * route_count]

    with jax.named_scope("slots"):
        fwd_slots = local_slots(
            fwd_routes_z, slot_positions(fwd_routes_z, expert_count), expert_class, class_count, capacity
        )
        bwd_slots = local_slots(
            bwd_routes_z, slot_positions(bwd_routes_z, expert_count), expert_class, class_count, capacity
        )

    with jax.named_scope("backward_experts"):
        bwd_table = slot_table(bwd_slots, slot_total)
        bwd_rows = swap_x(pack_rows(bwd_tok_z, bwd_table), x_count)
        grad_rows = swap_x(pack_rows(bwd_grads_z, bwd_table), x_count)
        bwd_res = backward_work(bwd_rows, grad_rows, w_up, w_down)

    with jax.named_scope("forward_experts"):
        fwd_table = slot_table(fwd_slots, slot_total)
        fwd_rows = swap_x(pack_rows(fwd_tok_z, fwd_table), x_count)
        fwd_rows, bwd_res = lax.optimization_barrier((fwd_rows, bwd_res))

    with jax.named_scope("forward_experts"):
        w_down_parts = [w_down[:, lo:hi] for lo, hi in cuts]
        fwd_res_parts = forward_work(fwd_rows, w_up, w_down_parts)

    with jax.named_scope("backward_experts"):
        bwd_back = swap_x(bwd_res, x_count)
        bwd_part = weighted_partial(bwd_back, bwd_slots, bwd_weights_z, slot_total)
        bwd_part, fwd_res_parts = lax.optimization_barrier((bwd_part, fwd_res_parts))
        bwd_out = sum_back(bwd_grads[0], bwd_part, z_index, jnp.bfloat16)

    with jax.named_scope("forward_experts"):
        next_parts = []
        for (lo, hi), fwd_res in zip(cuts, fwd_res_parts):
            fwd_back = swap_x(fwd_res, x_count)
            fwd_part = weighted_partial(fwd_back, fwd_slots, fwd_weights_z, slot_total)
            if not next_parts:
                bwd_out, fwd_part = lax.optimization_barrier((bwd_out, fwd_part))
                prev_grad = from_behind(bwd_out[None], "pp", -1)
            fwd_out = sum_back(fwd_tokens[0][:, lo:hi], fwd_part, z_index, jnp.bfloat16)
            next_parts.append(from_behind(fwd_out[None], "pp", 1))
        next_input = jnp.concatenate(next_parts, axis=-1)

    return (next_input, prev_grad)


def solution(mesh):
    devices = mesh.devices
    pp_count, ep_count = devices.shape
    split_mesh = Mesh(devices.reshape(pp_count, ep_count // Z_PARTS, Z_PARTS), ("pp", "ex", "ez"))
    rows = P("pp", ("ex", "ez"), None)
    placed = (rows, rows, rows, rows, rows, rows, rows, P("pp", None, ("ex", "ez")), rows)
    return jax.shard_map(
        on_device,
        mesh=split_mesh,
        in_specs=placed,
        out_specs=(rows, rows),
        check_vma=False,
    )
```

```python
import jax
import jax.numpy as jnp
from jax import lax
from jax.sharding import Mesh
from jax.sharding import PartitionSpec as P

Z_PARTS = 4
D_PARTS = 1


def from_behind(value, axis, by):
    size = lax.axis_size(axis)
    return lax.ppermute(value, axis, [(i, (i + by) % size) for i in range(size)])


def silu_slope(pre_act):
    sigmoid_value = jax.nn.sigmoid(pre_act)
    return sigmoid_value * (1.0 + pre_act * (1.0 - sigmoid_value))


def slot_positions(chosen, expert_count):
    groups, tok_rows, route_count = chosen.shape
    onehot = (chosen[..., None] == jnp.arange(expert_count, dtype=jnp.int32)).astype(jnp.int32)
    flat_hot = onehot.reshape(groups, tok_rows * route_count, expert_count)
    earlier = jnp.cumsum(flat_hot, axis=1) - flat_hot
    return jnp.sum(earlier * flat_hot, axis=2).reshape(groups, tok_rows, route_count)


def local_slots(chosen, position, expert_class, class_count, capacity):
    groups = chosen.shape[0]
    column = chosen // class_count
    mine = (chosen % class_count) == expert_class
    group = jnp.arange(groups, dtype=jnp.int32)[:, None, None]
    return jnp.where(mine, (column * groups + group) * capacity + position, -1)


def slot_table(slots, slot_total):
    flat = slots.reshape(-1, slots.shape[-1])
    return jnp.sum((flat[..., None] == jnp.arange(slot_total, dtype=jnp.int32)).astype(jnp.bfloat16), axis=1)


def pack_rows(member, table):
    flat = member.reshape(-1, member.shape[-1])
    return lax.dot_general(
        table, flat, (((0,), (0,)), ((), ())), preferred_element_type=jnp.float32
    ).astype(jnp.bfloat16)


def weighted_partial(results, slots, route_weights, slot_total):
    groups, tok_rows, route_count = slots.shape
    places = jnp.arange(slot_total, dtype=jnp.int32)
    total = None
    for k in range(route_count):
        table = (slots[:, :, k].reshape(-1, 1) == places).astype(jnp.bfloat16)
        picked = jnp.dot(table, results, preferred_element_type=jnp.float32)
        term = route_weights[:, :, k].reshape(-1, 1) * picked
        total = term if total is None else total + term
    return total.reshape(groups, tok_rows, -1)


def forward_work(rows, w_up, w_down_parts):
    hidden = jax.nn.silu(jnp.dot(rows, w_up, preferred_element_type=jnp.float32)).astype(jnp.bfloat16)
    return [jnp.dot(hidden, part, preferred_element_type=jnp.float32).astype(jnp.bfloat16) for part in w_down_parts]


def backward_work(rows, grad_rows, w_up, w_down):
    pre_act = jnp.dot(rows, w_up, preferred_element_type=jnp.float32)
    upstream = lax.dot_general(grad_rows, w_down, (((1,), (1,)), ((), ())), preferred_element_type=jnp.float32)
    hidden_grad = (silu_slope(pre_act) * upstream).astype(jnp.bfloat16)
    return lax.dot_general(
        hidden_grad, w_up, (((1,), (1,)), ((), ())), preferred_element_type=jnp.float32
    ).astype(jnp.bfloat16)


def swap_x(rows, x_count):
    spread = rows.reshape((x_count, -1) + rows.shape[1:])
    got = lax.all_to_all(spread, "ex", split_axis=0, concat_axis=0, tiled=True)
    return got.reshape(rows.shape)


def sum_back(residual, partial, z_index, wire_type):
    if wire_type == jnp.float32:
        own = (jnp.arange(partial.shape[0]) == z_index)[:, None, None]
        partial = partial + jnp.where(own, residual.astype(jnp.float32)[None], 0.0)
        total = lax.psum_scatter(partial, "ez", scatter_dimension=0, tiled=False)
    else:
        summed = lax.psum_scatter(partial.astype(wire_type), "ez", scatter_dimension=0, tiled=False)
        total = residual.astype(jnp.float32) + summed.astype(jnp.float32)
    return total.astype(jnp.bfloat16)


def on_device(
    fwd_tokens,
    fwd_routes,
    fwd_weights,
    bwd_tokens,
    bwd_grads,
    bwd_routes,
    bwd_weights,
    up_proj,
    down_proj,
):
    x_count = lax.axis_size("ex")
    z_count = lax.axis_size("ez")
    ep_count = x_count * z_count
    expert_count = ep_count // 2
    class_count = expert_count // x_count
    tok_rows = fwd_tokens.shape[1]
    route_count = fwd_routes.shape[2]
    capacity = 3 * tok_rows * route_count // ep_count
    slot_total = x_count * z_count * capacity
    z_index = lax.axis_index("ez")
    expert_class = z_index // (z_count // class_count)
    w_up = up_proj[0]
    w_down = down_proj[0]

    def gather_z(value):
        return lax.all_gather(value[0], "ez", axis=0, tiled=False)

    features = fwd_tokens.shape[-1]
    cuts = [(i * features // D_PARTS, (i + 1) * features // D_PARTS) for i in range(D_PARTS)]

    with jax.named_scope("gather_along_z"):
        bwd_tok_z = gather_z(bwd_tokens)
        bwd_grads_z = gather_z(bwd_grads)
        fwd_tokens_in, bwd_grads_z = lax.optimization_barrier((fwd_tokens, bwd_grads_z))
        fwd_tok_z = gather_z(fwd_tokens_in)
        meta = jnp.concatenate(
            [fwd_routes.astype(jnp.float32), fwd_weights, bwd_routes.astype(jnp.float32), bwd_weights], axis=-1
        )
        meta_z = gather_z(meta)
        fwd_routes_z = meta_z[:, :, 0:route_count].astype(jnp.int32)
        fwd_weights_z = meta_z[:, :, route_count : 2 * route_count]
        bwd_routes_z = meta_z[:, :, 2 * route_count : 3 * route_count].astype(jnp.int32)
        bwd_weights_z = meta_z[:, :, 3 * route_count : 4 * route_count]

    with jax.named_scope("slots"):
        fwd_slots = local_slots(
            fwd_routes_z, slot_positions(fwd_routes_z, expert_count), expert_class, class_count, capacity
        )
        bwd_slots = local_slots(
            bwd_routes_z, slot_positions(bwd_routes_z, expert_count), expert_class, class_count, capacity
        )

    with jax.named_scope("backward_experts"):
        bwd_table = slot_table(bwd_slots, slot_total)
        bwd_rows = swap_x(pack_rows(bwd_tok_z, bwd_table), x_count)
        grad_rows = swap_x(pack_rows(bwd_grads_z, bwd_table), x_count)
        bwd_res = backward_work(bwd_rows, grad_rows, w_up, w_down)

    with jax.named_scope("backward_experts"):
        bwd_back = swap_x(bwd_res, x_count)
        bwd_back, fwd_tok_z = lax.optimization_barrier((bwd_back, fwd_tok_z))
        bwd_part = weighted_partial(bwd_back, bwd_slots, bwd_weights_z, slot_total)
        bwd_out = sum_back(bwd_grads[0], bwd_part, z_index, jnp.bfloat16)

    with jax.named_scope("forward_experts"):
        fwd_table = slot_table(fwd_slots, slot_total)
        fwd_rows = swap_x(pack_rows(fwd_tok_z, fwd_table), x_count)
        w_down_parts = [w_down[:, lo:hi] for lo, hi in cuts]
        fwd_res_parts = forward_work(fwd_rows, w_up, w_down_parts)

    with jax.named_scope("forward_experts"):
        next_parts = []
        for (lo, hi), fwd_res in zip(cuts, fwd_res_parts):
            fwd_back = swap_x(fwd_res, x_count)
            fwd_part = weighted_partial(fwd_back, fwd_slots, fwd_weights_z, slot_total)
            if not next_parts:
                bwd_out, fwd_part = lax.optimization_barrier((bwd_out, fwd_part))
                prev_grad = from_behind(bwd_out[None], "pp", -1)
            fwd_out = sum_back(fwd_tokens[0][:, lo:hi], fwd_part, z_index, jnp.bfloat16)
            next_parts.append(from_behind(fwd_out[None], "pp", 1))
        next_input = jnp.concatenate(next_parts, axis=-1)

    return (next_input, prev_grad)


def solution(mesh):
    devices = mesh.devices
    pp_count, ep_count = devices.shape
    split_mesh = Mesh(devices.reshape(pp_count, ep_count // Z_PARTS, Z_PARTS), ("pp", "ex", "ez"))
    rows = P("pp", ("ex", "ez"), None)
    placed = (rows, rows, rows, rows, rows, rows, rows, P("pp", None, ("ex", "ez")), rows)
    return jax.shard_map(
        on_device,
        mesh=split_mesh,
        in_specs=placed,
        out_specs=(rows, rows),
        check_vma=False,
    )
```

```python
import jax
import jax.numpy as jnp
from jax import lax
from jax.sharding import Mesh
from jax.sharding import PartitionSpec as P

Z_PARTS = 4
D_PARTS = 1


def from_behind(value, axis, by):
    size = lax.axis_size(axis)
    return lax.ppermute(value, axis, [(i, (i + by) % size) for i in range(size)])


def silu_slope(pre_act):
    sigmoid_value = jax.nn.sigmoid(pre_act)
    return sigmoid_value * (1.0 + pre_act * (1.0 - sigmoid_value))


def slot_positions(chosen, expert_count):
    groups, tok_rows, route_count = chosen.shape
    onehot = (chosen[..., None] == jnp.arange(expert_count, dtype=jnp.int32)).astype(jnp.int32)
    flat_hot = onehot.reshape(groups, tok_rows * route_count, expert_count)
    earlier = jnp.cumsum(flat_hot, axis=1) - flat_hot
    return jnp.sum(earlier * flat_hot, axis=2).reshape(groups, tok_rows, route_count)


def local_slots(chosen, position, expert_class, class_count, capacity):
    groups = chosen.shape[0]
    column = chosen // class_count
    mine = (chosen % class_count) == expert_class
    group = jnp.arange(groups, dtype=jnp.int32)[:, None, None]
    return jnp.where(mine, (column * groups + group) * capacity + position, -1)


def slot_table(slots, slot_total):
    flat = slots.reshape(-1, slots.shape[-1])
    return jnp.sum((flat[..., None] == jnp.arange(slot_total, dtype=jnp.int32)).astype(jnp.bfloat16), axis=1)


def pack_rows(member, table):
    flat = member.reshape(-1, member.shape[-1])
    return lax.dot_general(
        table, flat, (((0,), (0,)), ((), ())), preferred_element_type=jnp.float32
    ).astype(jnp.bfloat16)


def weighted_partial(results, slots, route_weights, slot_total):
    groups, tok_rows, route_count = slots.shape
    places = jnp.arange(slot_total, dtype=jnp.int32)
    total = None
    for k in range(route_count):
        table = (slots[:, :, k].reshape(-1, 1) == places).astype(jnp.bfloat16)
        picked = jnp.dot(table, results, preferred_element_type=jnp.float32)
        term = route_weights[:, :, k].reshape(-1, 1) * picked
        total = term if total is None else total + term
    return total.reshape(groups, tok_rows, -1)


def forward_work(rows, w_up, w_down_parts):
    hidden = jax.nn.silu(jnp.dot(rows, w_up, preferred_element_type=jnp.float32)).astype(jnp.bfloat16)
    return [jnp.dot(hidden, part, preferred_element_type=jnp.float32).astype(jnp.bfloat16) for part in w_down_parts]


def backward_work(rows, grad_rows, w_up, w_down):
    pre_act = jnp.dot(rows, w_up, preferred_element_type=jnp.float32)
    upstream = lax.dot_general(grad_rows, w_down, (((1,), (1,)), ((), ())), preferred_element_type=jnp.float32)
    hidden_grad = (silu_slope(pre_act) * upstream).astype(jnp.bfloat16)
    return lax.dot_general(
        hidden_grad, w_up, (((1,), (1,)), ((), ())), preferred_element_type=jnp.float32
    ).astype(jnp.bfloat16)


def swap_x(rows, x_count):
    spread = rows.reshape((x_count, -1) + rows.shape[1:])
    got = lax.all_to_all(spread, "ex", split_axis=0, concat_axis=0, tiled=True)
    return got.reshape(rows.shape)


def sum_back(residual, partial, z_index, wire_type):
    if wire_type == jnp.float32:
        own = (jnp.arange(partial.shape[0]) == z_index)[:, None, None]
        partial = partial + jnp.where(own, residual.astype(jnp.float32)[None], 0.0)
        total = lax.psum_scatter(partial, "ez", scatter_dimension=0, tiled=False)
    else:
        summed = lax.psum_scatter(partial.astype(wire_type), "ez", scatter_dimension=0, tiled=False)
        total = residual.astype(jnp.float32) + summed.astype(jnp.float32)
    return total.astype(jnp.bfloat16)


def on_device(
    fwd_tokens,
    fwd_routes,
    fwd_weights,
    bwd_tokens,
    bwd_grads,
    bwd_routes,
    bwd_weights,
    up_proj,
    down_proj,
):
    x_count = lax.axis_size("ex")
    z_count = lax.axis_size("ez")
    ep_count = x_count * z_count
    expert_count = ep_count // 2
    class_count = expert_count // x_count
    tok_rows = fwd_tokens.shape[1]
    route_count = fwd_routes.shape[2]
    capacity = 3 * tok_rows * route_count // ep_count
    slot_total = x_count * z_count * capacity
    z_index = lax.axis_index("ez")
    expert_class = z_index // (z_count // class_count)
    w_up = up_proj[0]
    w_down = down_proj[0]
    fwd_w_up = from_behind(up_proj, "pp", 1)[0]
    fwd_w_down = from_behind(down_proj, "pp", 1)[0]
    fwd_tokens = from_behind(fwd_tokens, "pp", 1)
    fwd_meta = from_behind(jnp.concatenate([fwd_routes.astype(jnp.float32), fwd_weights], axis=-1), "pp", 1)
    fwd_routes = fwd_meta[:, :, 0 : fwd_routes.shape[2]].astype(jnp.int32)
    fwd_weights = fwd_meta[:, :, fwd_routes.shape[2] :]

    def gather_z(value):
        return lax.all_gather(value[0], "ez", axis=0, tiled=False)

    features = fwd_tokens.shape[-1]
    cuts = [(i * features // D_PARTS, (i + 1) * features // D_PARTS) for i in range(D_PARTS)]

    with jax.named_scope("gather_along_z"):
        bwd_tok_z = gather_z(bwd_tokens)
        bwd_grads_z = gather_z(bwd_grads)
        fwd_tokens_in, bwd_grads_z = lax.optimization_barrier((fwd_tokens, bwd_grads_z))
        fwd_tok_z = gather_z(fwd_tokens_in)
        meta = jnp.concatenate(
            [fwd_routes.astype(jnp.float32), fwd_weights, bwd_routes.astype(jnp.float32), bwd_weights], axis=-1
        )
        meta_z = gather_z(meta)
        fwd_routes_z = meta_z[:, :, 0:route_count].astype(jnp.int32)
        fwd_weights_z = meta_z[:, :, route_count : 2 * route_count]
        bwd_routes_z = meta_z[:, :, 2 * route_count : 3 * route_count].astype(jnp.int32)
        bwd_weights_z = meta_z[:, :, 3 * route_count : 4 * route_count]

    with jax.named_scope("slots"):
        fwd_slots = local_slots(
            fwd_routes_z, slot_positions(fwd_routes_z, expert_count), expert_class, class_count, capacity
        )
        bwd_slots = local_slots(
            bwd_routes_z, slot_positions(bwd_routes_z, expert_count), expert_class, class_count, capacity
        )

    with jax.named_scope("backward_experts"):
        bwd_table = slot_table(bwd_slots, slot_total)
        bwd_rows = swap_x(pack_rows(bwd_tok_z, bwd_table), x_count)
        fwd_w_up, fwd_w_down, bwd_rows = lax.optimization_barrier((fwd_w_up, fwd_w_down, bwd_rows))
        grad_rows = swap_x(pack_rows(bwd_grads_z, bwd_table), x_count)
        bwd_res = backward_work(bwd_rows, grad_rows, w_up, w_down)

    with jax.named_scope("forward_experts"):
        fwd_table = slot_table(fwd_slots, slot_total)
        fwd_rows = swap_x(pack_rows(fwd_tok_z, fwd_table), x_count)
        fwd_rows, bwd_res = lax.optimization_barrier((fwd_rows, bwd_res))

    with jax.named_scope("forward_experts"):
        w_down_parts = [fwd_w_down[:, lo:hi] for lo, hi in cuts]
        fwd_res_parts = forward_work(fwd_rows, fwd_w_up, w_down_parts)

    with jax.named_scope("backward_experts"):
        bwd_back = swap_x(bwd_res, x_count)
        bwd_part = weighted_partial(bwd_back, bwd_slots, bwd_weights_z, slot_total)
        bwd_part, fwd_res_parts = lax.optimization_barrier((bwd_part, fwd_res_parts))
        bwd_out = sum_back(bwd_grads[0], bwd_part, z_index, jnp.bfloat16)

    with jax.named_scope("forward_experts"):
        next_parts = []
        for (lo, hi), fwd_res in zip(cuts, fwd_res_parts):
            fwd_back = swap_x(fwd_res, x_count)
            fwd_part = weighted_partial(fwd_back, fwd_slots, fwd_weights_z, slot_total)
            if not next_parts:
                bwd_out, fwd_part = lax.optimization_barrier((bwd_out, fwd_part))
                prev_grad = from_behind(bwd_out[None], "pp", -1)
            fwd_out = sum_back(fwd_tokens[0][:, lo:hi], fwd_part, z_index, jnp.bfloat16)
            next_parts.append(fwd_out[None])
        next_input = jnp.concatenate(next_parts, axis=-1)

    return (next_input, prev_grad)


def solution(mesh):
    devices = mesh.devices
    pp_count, ep_count = devices.shape
    split_mesh = Mesh(devices.reshape(pp_count, ep_count // Z_PARTS, Z_PARTS), ("pp", "ex", "ez"))
    rows = P("pp", ("ex", "ez"), None)
    placed = (rows, rows, rows, rows, rows, rows, rows, P("pp", None, ("ex", "ez")), rows)
    return jax.shard_map(
        on_device,
        mesh=split_mesh,
        in_specs=placed,
        out_specs=(rows, rows),
        check_vma=False,
    )
```

```python
import jax
import jax.numpy as jnp
from jax import lax
from jax.sharding import Mesh
from jax.sharding import PartitionSpec as P

Z_PARTS = 4
D_PARTS = 1


def from_behind(value, axis, by):
    size = lax.axis_size(axis)
    return lax.ppermute(value, axis, [(i, (i + by) % size) for i in range(size)])


def silu_slope(pre_act):
    sigmoid_value = jax.nn.sigmoid(pre_act)
    return sigmoid_value * (1.0 + pre_act * (1.0 - sigmoid_value))


def slot_positions(chosen, expert_count):
    groups, tok_rows, route_count = chosen.shape
    onehot = (chosen[..., None] == jnp.arange(expert_count, dtype=jnp.int32)).astype(jnp.int32)
    flat_hot = onehot.reshape(groups, tok_rows * route_count, expert_count)
    earlier = jnp.cumsum(flat_hot, axis=1) - flat_hot
    return jnp.sum(earlier * flat_hot, axis=2).reshape(groups, tok_rows, route_count)


def local_slots(chosen, position, expert_class, class_count, capacity):
    groups = chosen.shape[0]
    column = chosen // class_count
    mine = (chosen % class_count) == expert_class
    group = jnp.arange(groups, dtype=jnp.int32)[:, None, None]
    return jnp.where(mine, (column * groups + group) * capacity + position, -1)


def slot_table(slots, slot_total):
    flat = slots.reshape(-1, slots.shape[-1])
    return jnp.sum((flat[..., None] == jnp.arange(slot_total, dtype=jnp.int32)).astype(jnp.bfloat16), axis=1)


def pack_rows(member, table):
    flat = member.reshape(-1, member.shape[-1])
    return lax.dot_general(
        table, flat, (((0,), (0,)), ((), ())), preferred_element_type=jnp.float32
    ).astype(jnp.bfloat16)


def weighted_partial(results, slots, route_weights, slot_total):
    groups, tok_rows, route_count = slots.shape
    places = jnp.arange(slot_total, dtype=jnp.int32)
    total = None
    for k in range(route_count):
        table = (slots[:, :, k].reshape(-1, 1) == places).astype(jnp.bfloat16)
        picked = jnp.dot(table, results, preferred_element_type=jnp.float32)
        term = route_weights[:, :, k].reshape(-1, 1) * picked
        total = term if total is None else total + term
    return total.reshape(groups, tok_rows, -1)


def forward_work(rows, w_up, w_down_parts):
    hidden = jax.nn.silu(jnp.dot(rows, w_up, preferred_element_type=jnp.float32)).astype(jnp.bfloat16)
    return [jnp.dot(hidden, part, preferred_element_type=jnp.float32).astype(jnp.bfloat16) for part in w_down_parts]


def backward_work(rows, grad_rows, w_up, w_down):
    pre_act = jnp.dot(rows, w_up, preferred_element_type=jnp.float32)
    upstream = lax.dot_general(grad_rows, w_down, (((1,), (1,)), ((), ())), preferred_element_type=jnp.float32)
    hidden_grad = (silu_slope(pre_act) * upstream).astype(jnp.bfloat16)
    return lax.dot_general(
        hidden_grad, w_up, (((1,), (1,)), ((), ())), preferred_element_type=jnp.float32
    ).astype(jnp.bfloat16)


def swap_x(rows, x_count):
    spread = rows.reshape((x_count, -1) + rows.shape[1:])
    got = lax.all_to_all(spread, "ex", split_axis=0, concat_axis=0, tiled=True)
    return got.reshape(rows.shape)


def sum_back(residual, partial, z_index, wire_type):
    if wire_type == jnp.float32:
        own = (jnp.arange(partial.shape[0]) == z_index)[:, None, None]
        partial = partial + jnp.where(own, residual.astype(jnp.float32)[None], 0.0)
        total = lax.psum_scatter(partial, "ez", scatter_dimension=0, tiled=False)
    else:
        summed = lax.psum_scatter(partial.astype(wire_type), "ez", scatter_dimension=0, tiled=False)
        total = residual.astype(jnp.float32) + summed.astype(jnp.float32)
    return total.astype(jnp.bfloat16)


def on_device(
    fwd_tokens,
    fwd_routes,
    fwd_weights,
    bwd_tokens,
    bwd_grads,
    bwd_routes,
    bwd_weights,
    up_proj,
    down_proj,
):
    x_count = lax.axis_size("ex")
    z_count = lax.axis_size("ez")
    ep_count = x_count * z_count
    expert_count = ep_count // 2
    class_count = expert_count // x_count
    tok_rows = fwd_tokens.shape[1]
    route_count = fwd_routes.shape[2]
    capacity = 3 * tok_rows * route_count // ep_count
    slot_total = x_count * z_count * capacity
    z_index = lax.axis_index("ez")
    expert_class = z_index // (z_count // class_count)
    w_up = up_proj[0]
    w_down = down_proj[0]
    fwd_w_up = from_behind(up_proj, "pp", 1)[0]
    fwd_w_down = from_behind(down_proj, "pp", 1)[0]
    fwd_tokens = from_behind(fwd_tokens, "pp", 1)
    fwd_meta = from_behind(jnp.concatenate([fwd_routes.astype(jnp.float32), fwd_weights], axis=-1), "pp", 1)
    fwd_routes = fwd_meta[:, :, 0 : fwd_routes.shape[2]].astype(jnp.int32)
    fwd_weights = fwd_meta[:, :, fwd_routes.shape[2] :]

    def gather_z(value):
        return lax.all_gather(value[0], "ez", axis=0, tiled=False)

    features = fwd_tokens.shape[-1]
    cuts = [(i * features // D_PARTS, (i + 1) * features // D_PARTS) for i in range(D_PARTS)]

    with jax.named_scope("gather_along_z"):
        bwd_tok_z = gather_z(bwd_tokens)
        bwd_grads_z = gather_z(bwd_grads)
        fwd_tokens_in, bwd_grads_z = lax.optimization_barrier((fwd_tokens, bwd_grads_z))
        fwd_tok_z = gather_z(fwd_tokens_in)
        meta = jnp.concatenate(
            [fwd_routes.astype(jnp.float32), fwd_weights, bwd_routes.astype(jnp.float32), bwd_weights], axis=-1
        )
        meta_z = gather_z(meta)
        fwd_routes_z = meta_z[:, :, 0:route_count].astype(jnp.int32)
        fwd_weights_z = meta_z[:, :, route_count : 2 * route_count]
        bwd_routes_z = meta_z[:, :, 2 * route_count : 3 * route_count].astype(jnp.int32)
        bwd_weights_z = meta_z[:, :, 3 * route_count : 4 * route_count]

    with jax.named_scope("slots"):
        fwd_slots = local_slots(
            fwd_routes_z, slot_positions(fwd_routes_z, expert_count), expert_class, class_count, capacity
        )
        bwd_slots = local_slots(
            bwd_routes_z, slot_positions(bwd_routes_z, expert_count), expert_class, class_count, capacity
        )

    with jax.named_scope("backward_experts"):
        bwd_table = slot_table(bwd_slots, slot_total)
        bwd_rows = swap_x(pack_rows(bwd_tok_z, bwd_table), x_count)
        fwd_w_up, fwd_w_down, bwd_grads_z = lax.optimization_barrier((fwd_w_up, fwd_w_down, bwd_grads_z))
        grad_rows = swap_x(pack_rows(bwd_grads_z, bwd_table), x_count)
        bwd_res = backward_work(bwd_rows, grad_rows, w_up, w_down)

    with jax.named_scope("forward_experts"):
        fwd_table = slot_table(fwd_slots, slot_total)
        fwd_rows = swap_x(pack_rows(fwd_tok_z, fwd_table), x_count)
        fwd_rows, bwd_res = lax.optimization_barrier((fwd_rows, bwd_res))

    with jax.named_scope("forward_experts"):
        w_down_parts = [fwd_w_down[:, lo:hi] for lo, hi in cuts]
        fwd_res_parts = forward_work(fwd_rows, fwd_w_up, w_down_parts)

    with jax.named_scope("backward_experts"):
        bwd_back = swap_x(bwd_res, x_count)
        bwd_part = weighted_partial(bwd_back, bwd_slots, bwd_weights_z, slot_total)
        bwd_part, fwd_res_parts = lax.optimization_barrier((bwd_part, fwd_res_parts))
        bwd_out = sum_back(bwd_grads[0], bwd_part, z_index, jnp.bfloat16)

    with jax.named_scope("forward_experts"):
        next_parts = []
        for (lo, hi), fwd_res in zip(cuts, fwd_res_parts):
            fwd_back = swap_x(fwd_res, x_count)
            fwd_part = weighted_partial(fwd_back, fwd_slots, fwd_weights_z, slot_total)
            if not next_parts:
                bwd_out, fwd_part = lax.optimization_barrier((bwd_out, fwd_part))
                prev_grad = from_behind(bwd_out[None], "pp", -1)
            fwd_out = sum_back(fwd_tokens[0][:, lo:hi], fwd_part, z_index, jnp.bfloat16)
            next_parts.append(fwd_out[None])
        next_input = jnp.concatenate(next_parts, axis=-1)

    return (next_input, prev_grad)


def solution(mesh):
    devices = mesh.devices
    pp_count, ep_count = devices.shape
    split_mesh = Mesh(devices.reshape(pp_count, ep_count // Z_PARTS, Z_PARTS), ("pp", "ex", "ez"))
    rows = P("pp", ("ex", "ez"), None)
    placed = (rows, rows, rows, rows, rows, rows, rows, P("pp", None, ("ex", "ez")), rows)
    return jax.shard_map(
        on_device,
        mesh=split_mesh,
        in_specs=placed,
        out_specs=(rows, rows),
        check_vma=False,
    )
```

```python
import jax
import jax.numpy as jnp
from jax import lax
from jax.sharding import Mesh
from jax.sharding import PartitionSpec as P

Z_PARTS = 4
D_PARTS = 1


def from_behind(value, axis, by):
    size = lax.axis_size(axis)
    return lax.ppermute(value, axis, [(i, (i + by) % size) for i in range(size)])


def silu_slope(pre_act):
    sigmoid_value = jax.nn.sigmoid(pre_act)
    return sigmoid_value * (1.0 + pre_act * (1.0 - sigmoid_value))


def slot_positions(chosen, expert_count):
    groups, tok_rows, route_count = chosen.shape
    onehot = (chosen[..., None] == jnp.arange(expert_count, dtype=jnp.int32)).astype(jnp.int32)
    flat_hot = onehot.reshape(groups, tok_rows * route_count, expert_count)
    earlier = jnp.cumsum(flat_hot, axis=1) - flat_hot
    return jnp.sum(earlier * flat_hot, axis=2).reshape(groups, tok_rows, route_count)


def local_slots(chosen, position, expert_class, class_count, capacity):
    groups = chosen.shape[0]
    column = chosen // class_count
    mine = (chosen % class_count) == expert_class
    group = jnp.arange(groups, dtype=jnp.int32)[:, None, None]
    return jnp.where(mine, (column * groups + group) * capacity + position, -1)


def slot_table(slots, slot_total):
    flat = slots.reshape(-1, slots.shape[-1])
    return jnp.sum((flat[..., None] == jnp.arange(slot_total, dtype=jnp.int32)).astype(jnp.bfloat16), axis=1)


def pack_rows(member, table):
    flat = member.reshape(-1, member.shape[-1])
    return lax.dot_general(
        table, flat, (((0,), (0,)), ((), ())), preferred_element_type=jnp.float32
    ).astype(jnp.bfloat16)


def weighted_partial(results, slots, route_weights, slot_total):
    groups, tok_rows, route_count = slots.shape
    places = jnp.arange(slot_total, dtype=jnp.int32)
    by_route = jnp.moveaxis(slots, 2, 0).reshape(route_count * groups * tok_rows, 1)
    table = (by_route == places).astype(jnp.bfloat16)
    picked = jnp.dot(table, results, preferred_element_type=jnp.float32).reshape(route_count, groups * tok_rows, -1)
    total = None
    for k in range(route_count):
        term = route_weights[:, :, k].reshape(-1, 1) * picked[k]
        total = term if total is None else total + term
    return total.reshape(groups, tok_rows, -1)


def forward_work(rows, w_up, w_down_parts):
    hidden = jax.nn.silu(jnp.dot(rows, w_up, preferred_element_type=jnp.float32)).astype(jnp.bfloat16)
    return [jnp.dot(hidden, part, preferred_element_type=jnp.float32).astype(jnp.bfloat16) for part in w_down_parts]


def backward_work(rows, grad_rows, w_up, w_down):
    pre_act = jnp.dot(rows, w_up, preferred_element_type=jnp.float32)
    upstream = lax.dot_general(grad_rows, w_down, (((1,), (1,)), ((), ())), preferred_element_type=jnp.float32)
    hidden_grad = (silu_slope(pre_act) * upstream).astype(jnp.bfloat16)
    return lax.dot_general(
        hidden_grad, w_up, (((1,), (1,)), ((), ())), preferred_element_type=jnp.float32
    ).astype(jnp.bfloat16)


def swap_x(rows, x_count):
    spread = rows.reshape((x_count, -1) + rows.shape[1:])
    got = lax.all_to_all(spread, "ex", split_axis=0, concat_axis=0, tiled=True)
    return got.reshape(rows.shape)


def sum_back(residual, partial, z_index, wire_type):
    if wire_type == jnp.float32:
        own = (jnp.arange(partial.shape[0]) == z_index)[:, None, None]
        partial = partial + jnp.where(own, residual.astype(jnp.float32)[None], 0.0)
        total = lax.psum_scatter(partial, "ez", scatter_dimension=0, tiled=False)
    else:
        summed = lax.psum_scatter(partial.astype(wire_type), "ez", scatter_dimension=0, tiled=False)
        total = residual.astype(jnp.float32) + summed.astype(jnp.float32)
    return total.astype(jnp.bfloat16)


def on_device(
    fwd_tokens,
    fwd_routes,
    fwd_weights,
    bwd_tokens,
    bwd_grads,
    bwd_routes,
    bwd_weights,
    up_proj,
    down_proj,
):
    x_count = lax.axis_size("ex")
    z_count = lax.axis_size("ez")
    ep_count = x_count * z_count
    expert_count = ep_count // 2
    class_count = expert_count // x_count
    tok_rows = fwd_tokens.shape[1]
    route_count = fwd_routes.shape[2]
    capacity = 3 * tok_rows * route_count // ep_count
    slot_total = x_count * z_count * capacity
    z_index = lax.axis_index("ez")
    expert_class = z_index // (z_count // class_count)
    w_up = up_proj[0]
    w_down = down_proj[0]

    def gather_z(value):
        return lax.all_gather(value[0], "ez", axis=0, tiled=False)

    features = fwd_tokens.shape[-1]
    cuts = [(i * features // D_PARTS, (i + 1) * features // D_PARTS) for i in range(D_PARTS)]

    with jax.named_scope("gather_along_z"):
        bwd_tok_z = gather_z(bwd_tokens)
        bwd_grads_z = gather_z(bwd_grads)
        fwd_tokens_in, bwd_grads_z = lax.optimization_barrier((fwd_tokens, bwd_grads_z))
        fwd_tok_z = gather_z(fwd_tokens_in)
        meta = jnp.concatenate(
            [fwd_routes.astype(jnp.float32), fwd_weights, bwd_routes.astype(jnp.float32), bwd_weights], axis=-1
        )
        meta_z = gather_z(meta)
        fwd_routes_z = meta_z[:, :, 0:route_count].astype(jnp.int32)
        fwd_weights_z = meta_z[:, :, route_count : 2 * route_count]
        bwd_routes_z = meta_z[:, :, 2 * route_count : 3 * route_count].astype(jnp.int32)
        bwd_weights_z = meta_z[:, :, 3 * route_count : 4 * route_count]

    with jax.named_scope("slots"):
        fwd_slots = local_slots(
            fwd_routes_z, slot_positions(fwd_routes_z, expert_count), expert_class, class_count, capacity
        )
        bwd_slots = local_slots(
            bwd_routes_z, slot_positions(bwd_routes_z, expert_count), expert_class, class_count, capacity
        )

    with jax.named_scope("backward_experts"):
        bwd_table = slot_table(bwd_slots, slot_total)
        bwd_rows = swap_x(pack_rows(bwd_tok_z, bwd_table), x_count)
        grad_rows = swap_x(pack_rows(bwd_grads_z, bwd_table), x_count)
        bwd_res = backward_work(bwd_rows, grad_rows, w_up, w_down)

    with jax.named_scope("forward_experts"):
        fwd_table = slot_table(fwd_slots, slot_total)
        fwd_rows = swap_x(pack_rows(fwd_tok_z, fwd_table), x_count)
        fwd_rows, bwd_res = lax.optimization_barrier((fwd_rows, bwd_res))

    with jax.named_scope("forward_experts"):
        w_down_parts = [w_down[:, lo:hi] for lo, hi in cuts]
        fwd_res_parts = forward_work(fwd_rows, w_up, w_down_parts)

    with jax.named_scope("backward_experts"):
        bwd_back = swap_x(bwd_res, x_count)
        bwd_part = weighted_partial(bwd_back, bwd_slots, bwd_weights_z, slot_total)
        bwd_part, fwd_res_parts = lax.optimization_barrier((bwd_part, fwd_res_parts))
        bwd_out = sum_back(bwd_grads[0], bwd_part, z_index, jnp.bfloat16)

    with jax.named_scope("forward_experts"):
        next_parts = []
        for (lo, hi), fwd_res in zip(cuts, fwd_res_parts):
            fwd_back = swap_x(fwd_res, x_count)
            fwd_part = weighted_partial(fwd_back, fwd_slots, fwd_weights_z, slot_total)
            if not next_parts:
                bwd_out, fwd_part = lax.optimization_barrier((bwd_out, fwd_part))
                prev_grad = from_behind(bwd_out[None], "pp", -1)
            fwd_out = sum_back(fwd_tokens[0][:, lo:hi], fwd_part, z_index, jnp.bfloat16)
            next_parts.append(from_behind(fwd_out[None], "pp", 1))
        next_input = jnp.concatenate(next_parts, axis=-1)

    return (next_input, prev_grad)


def solution(mesh):
    devices = mesh.devices
    pp_count, ep_count = devices.shape
    split_mesh = Mesh(devices.reshape(pp_count, ep_count // Z_PARTS, Z_PARTS), ("pp", "ex", "ez"))
    rows = P("pp", ("ex", "ez"), None)
    placed = (rows, rows, rows, rows, rows, rows, rows, P("pp", None, ("ex", "ez")), rows)
    return jax.shard_map(
        on_device,
        mesh=split_mesh,
        in_specs=placed,
        out_specs=(rows, rows),
        check_vma=False,
    )
```
